32 devices in a mesh: group: 4 (over y, x), dom: 8 (over z, core).
Axes of the slice: x: 2, y: 2, z: 4, core: 2. Of those that a mesh axis runs over, the one named last changes fastest.
Arguments:
- pin_feats: bfloat16 [32768, 256], P(('group', 'dom')), may hold values from -6 to 6
- w_self: bfloat16 [256, 256], replicated, may hold values from -0.375 to 0.375
- w_edge: bfloat16 [4, 256, 256], replicated, may hold values from -0.375 to 0.375
- w_head: bfloat16 [256, 1024], replicated, may hold values from -0.375 to 0.375
- w_out: bfloat16 [1024], replicated, may hold values from -0.1875 to 0.1875
- send_rows: int32 [32, 512], P(('group', 'dom')), may hold values from 0 to 1023
- edge_src: int32 [32, 4, 1024], P(('group', 'dom')), may hold values from 0 to 1535
- edge_dst: int32 [32, 4, 1024], P(('group', 'dom')), may hold values from 0 to 1023
- pin_owner: int32 [32768, 1], P(('group', 'dom')), may hold values from 0 to 31; in each aligned block of 1024 rows (0 to 1023, 1024 to 2047, ...) at most 64 rows name the same one
- pin_net: int32 [32768], P(('group', 'dom')), may hold values from 0 to 255
- net_target: float32 [8192], P(('group', 'dom')), may hold values from -6 to 6
Outputs:
- prediction: float32 [8192], P(('group', 'dom'))
- grad_feats: bfloat16 [32768, 256], P(('group', 'dom'))
- grad_self: float32 [256, 256], replicated
- grad_edge: float32 [4, 256, 256], replicated
- grad_head: float32 [256, 1024], replicated
- grad_out: float32 [1024], replicated
The draws below stay inside these ranges and needn't reach their ends.
Inputs may be any that keep to these rules, and one draw needn't show every extreme that they name: `pin_owner`: among the pins of one device at most 64 name one owner, and in every draw some device sends exactly 64 pins to some owner.
All inputs are finite; a program needn't handle non-finite values.
Results may differ from the reference program's by a relative error of at most 0.0094.
Values may be sent and summed in bfloat16 or wider, within the bound.
No kernel may reach another device: no remote copies, remote signals or barrier semaphores. Data moves between devices by JAX's collectives and lax.ppermute only.
A program may use at most 64 MiB of HBM per device.

```python
import math
import jax
import jax.numpy as jnp
import numpy as np
from jax import lax

D = 256
HEAD = 1024
ETYPES = 4
PINS_DEV = 1024
EPT = 1024
HALO = 256
NETS_DEV = 256
CAP = 64
PINS = 32768
NETS = 8192
N_GROUP = 4
N_DOM = 8
DEVICES = 32


def plant(entries, own_key, low, high):
    longest = entries.shape.index(max(entries.shape))
    spots = []
    for shift in (0, 1):
        where = [jax.random.randint(jax.random.fold_in(own_key, axis), (), 0, length) for axis, length in enumerate(entries.shape)]
        where[longest] = (where[longest] + shift) % entries.shape[longest]
        spots.append(tuple(where))
    return entries.at[spots[0]].set(low).at[spots[1]].set(high)


def steps_of(stream_key, shape, pieces, smallest, high):
    def one(axis_at, blocks):
        steps = jax.random.uniform(jax.random.fold_in(jax.random.fold_in(stream_key, 6), axis_at), (blocks,), jnp.float32, smallest / len(pieces), high / len(pieces))
        return jnp.repeat(jnp.exp(steps), shape[axis_at] // blocks).reshape((-1,) + (1,) * (len(shape) - axis_at - 1))

    gain = one(*pieces[0])
    for cut in pieces[1:]:
        gain = gain * one(*cut)
    return gain


def assign_block(key, own, number, rows, count, top, reach, lean):
    ranking = jax.random.permutation(key, count)
    packed, common = shares(count, rows * top, reach, lean, True), shares(count, rows * top, reach, lean, False)
    places = jnp.arange(count)

    def named(lengths, turn):
        used = int((lengths > 0).sum())
        fixed = max(1, used // 4)
        shifted = fixed + (places - fixed + turn * (used - fixed)) % max(1, count - fixed)
        return jnp.zeros((count,), jnp.int32).at[ranking[jnp.where(places < fixed, places, shifted)]].set(jnp.asarray(lengths, jnp.int32))

    lengths = jnp.where(number % 4 == 0, named(packed, number // 4), named(common, number - number // 4 - 1))
    mixed = jax.random.permutation(jax.random.fold_in(own, 3), count)
    donor, receiver = mixed[0:count // 2 * 2:2], mixed[1:count // 2 * 2:2]
    room = jnp.minimum(lengths[donor] - 1, reach - lengths[receiver]) // 2
    room = jnp.where((donor == ranking[0]) | (receiver == ranking[0]) | (lengths[receiver] == 0), 0, jnp.maximum(room, 0))
    shifted = jax.random.randint(jax.random.fold_in(own, 4), (count // 2,), 0, 1 << 20) % (room + 1)
    lengths = lengths.at[donor].add(-shifted).at[receiver].add(shifted)
    labels = jnp.searchsorted(jnp.cumsum(lengths), jnp.arange(rows * top), side="right").astype(jnp.int32)
    listing = labels.reshape(top, rows).T
    listing = listing[jax.random.permutation(jax.random.fold_in(own, 1), rows)]
    turn = jax.random.randint(jax.random.fold_in(own, 2), (rows, 1), 0, top)
    return jnp.take_along_axis(listing, (jnp.arange(top)[None, :] + turn) % top, axis=1)


def shares(count, total, bound, skew, full):
    weights = [(1 << 20) // math.isqrt(grade ** skew) + 1 for grade in range(1, count + 1)]
    largest = bound if full else min(bound, max(-(-total // count), total * weights[0] // sum(weights)))
    least = 1 if total - largest >= count - 1 else 0
    counts, rest = [largest] + [least] * (count - 1), total - largest - least * (count - 1)
    while rest > 0:
        free = [i for i in range(1, count) if counts[i] < largest] or [i for i in range(1, count) if counts[i] < bound]
        pool, left = sum([weights[i] for i in free]), rest
        for i in free:
            addition = min(bound - counts[i], max(1, left * weights[i] // pool), rest)
            counts[i] = counts[i] + addition
            rest = rest - addition
    return np.array(counts)


def bell_draw(own_key, dims, deviation, reach, split=(), kind=jnp.bfloat16):
    factor_of = steps_of(own_key, dims, split, -0.22, 0.18) if split else 1.0
    result = jax.random.normal(own_key, dims, jnp.float32) * deviation * factor_of
    return jnp.minimum(jnp.maximum(result, -reach), reach).astype(kind)


def setup_inputs(seed: int = 0) -> dict:
    key_of = jax.random.split(jax.random.key(seed), 12)
    pin_feats = bell_draw(key_of[0], (PINS, D), 1.0, 6.0, ((0, 32),))
    w_self = bell_draw(key_of[1], (D, D), D ** -0.5, 0.375)
    w_edge = bell_draw(key_of[2], (ETYPES, D, D), D ** -0.5, 0.375)
    w_head = bell_draw(key_of[3], (D, HEAD), D ** -0.5, 0.375)
    w_out = bell_draw(key_of[4], (HEAD,), HEAD ** -0.5, 0.1875)
    send_rows = plant(jax.random.randint(key_of[5], (DEVICES, 2 * HALO), 0, PINS_DEV), jax.random.fold_in(key_of[5], 1), 0, PINS_DEV - 1).astype(jnp.int32)
    edge_src = plant(jax.random.randint(key_of[6], (DEVICES, ETYPES, EPT), 0, PINS_DEV + 2 * HALO), jax.random.fold_in(key_of[6], 1), 0, (PINS_DEV + 2 * HALO) - 1).astype(jnp.int32)
    edge_dst = plant(jax.random.randint(key_of[7], (DEVICES, ETYPES, EPT), 0, PINS_DEV), jax.random.fold_in(key_of[7], 1), 0, PINS_DEV - 1).astype(jnp.int32)
    pin_owner_keys = jax.random.split(jax.random.fold_in(key_of[8], 1), PINS // PINS_DEV)
    pin_owner_turns = jax.random.permutation(jax.random.fold_in(key_of[8], 3), PINS // PINS_DEV)
    pin_owner = jax.vmap(lambda own, number: assign_block(jax.random.fold_in(key_of[8], 2), own, number, PINS_DEV, DEVICES, 1, CAP, 2))(pin_owner_keys, pin_owner_turns).reshape((PINS, 1))
    pin_net = plant(jax.random.randint(key_of[9], (PINS,), 0, NETS_DEV), jax.random.fold_in(key_of[9], 1), 0, NETS_DEV - 1).astype(jnp.int32)
    net_target = bell_draw(key_of[10], (NETS,), 1.0, 6.0, ((0, 32),), jnp.float32)
    return dict(pin_feats=pin_feats, w_self=w_self, w_edge=w_edge, w_head=w_head, w_out=w_out, send_rows=send_rows, edge_src=edge_src, edge_dst=edge_dst, pin_owner=pin_owner, pin_net=pin_net, net_target=net_target)


def silu_slope(values):
    sigma_val = jax.nn.sigmoid(values)
    return sigma_val * (1.0 + values * (1.0 - sigma_val))

def neighbour_rows(halo_parts):
    feat_width = halo_parts.shape[-1]
    device_grid = halo_parts.reshape(N_GROUP, N_DOM, 2 * HALO, feat_width)
    zero_rim = jnp.zeros((N_GROUP, 1, HALO, feat_width), halo_parts.dtype)
    from_left = jnp.concatenate([zero_rim, device_grid[:, :-1, HALO:]], 1)
    from_right = jnp.concatenate([device_grid[:, 1:, :HALO], zero_rim], 1)
    return jnp.concatenate([from_left, from_right], 2).reshape(N_GROUP * N_DOM, 2 * HALO, feat_width)

def forward_pass(feats_one, halo_one, sources, endpoints, w_self, w_edge):
    node_table = jnp.concatenate([feats_one, halo_one], 0)
    gathered = node_table[sources]
    message = jnp.einsum('tek,tkd->ted', gathered.astype(jnp.float32), w_edge.astype(jnp.float32))
    flat_end = endpoints.reshape(-1)
    summed = jnp.zeros((PINS_DEV, D), jnp.float32).at[flat_end].add(message.reshape(-1, D))
    degree = jnp.zeros((PINS_DEV,), jnp.float32).at[flat_end].add(jnp.ones(flat_end.shape, jnp.float32))
    inverse = 1.0 / (1.0 + degree)
    preact = jnp.dot(feats_one, w_self, preferred_element_type=jnp.float32) + summed * inverse[:, None]
    return (gathered, inverse, preact)

def reference(pin_feats, w_self, w_edge, w_head, w_out, send_rows, edge_src, edge_dst, pin_owner, pin_net, net_target):
    devices_all = N_GROUP * N_DOM
    feats_dev = pin_feats.reshape(devices_all, PINS_DEV, D)
    outgoing = jax.vmap(lambda rows_one, list_one: rows_one[list_one])(feats_dev, send_rows)
    halos = neighbour_rows(outgoing)

    def first_pass(record):
        feats_one, halo_one, sources, endpoints = record
        unused_a, unused_b, preact = forward_pass(feats_one, halo_one, sources, endpoints, w_self, w_edge)
        return jax.nn.silu(preact).astype(jnp.bfloat16)
    hidden = lax.map(first_pass, (feats_dev, halos, edge_src, edge_dst))
    net_rows = (pin_owner[:, 0].astype(jnp.int32) * NETS_DEV + pin_net.astype(jnp.int32)).reshape(devices_all, PINS_DEV)

    def pool_step(running, record):
        rows_one, index_one = record
        return (running.at[index_one].add(rows_one.astype(jnp.float32)), None)
    pooled, unused_c = lax.scan(pool_step, jnp.zeros((NETS, D), jnp.float32), (hidden, net_rows))

    def head_step(carry, record):
        emb_block, target_block = record
        pooled_b = emb_block.astype(jnp.bfloat16)
        head_pre = jnp.dot(pooled_b, w_head, preferred_element_type=jnp.float32)
        activated = jax.nn.silu(head_pre).astype(jnp.bfloat16)
        predicted = jnp.dot(activated, w_out, preferred_element_type=jnp.float32)
        misfit = predicted - target_block
        head_grad = (misfit[:, None] * w_out.astype(jnp.float32)[None, :] * silu_slope(head_pre)).astype(jnp.bfloat16)
        head_sum = jnp.einsum('nd,nh->dh', pooled_b.astype(jnp.float32), head_grad.astype(jnp.float32))
        out_sum = jnp.dot(misfit, activated.astype(jnp.float32), precision=lax.Precision.HIGHEST)
        net_grad = jnp.dot(head_grad, w_head.T, preferred_element_type=jnp.float32).astype(jnp.bfloat16)
        return ((carry[0] + head_sum, carry[1] + out_sum), (predicted, net_grad))
    start_carry = (jnp.zeros((D, HEAD), jnp.float32), jnp.zeros((HEAD,), jnp.float32))
    (head_total, out_total), (predicted, net_grad) = lax.scan(head_step, start_carry, (pooled.reshape(devices_all, NETS_DEV, D), net_target.reshape(devices_all, NETS_DEV)))
    net_grad = net_grad.reshape(NETS, D)

    def second_pass(record):
        feats_one, halo_one, sources, endpoints, index_one = record
        gathered, inverse, preact = forward_pass(feats_one, halo_one, sources, endpoints, w_self, w_edge)
        pin_grad = net_grad[index_one]
        preact_grad = (pin_grad.astype(jnp.float32) * silu_slope(preact)).astype(jnp.bfloat16)
        self_sum = jnp.einsum('pk,pd->kd', feats_one.astype(jnp.float32), preact_grad.astype(jnp.float32))
        agg_grad = (preact_grad.astype(jnp.float32) * inverse[:, None]).astype(jnp.bfloat16)
        edge_rows = agg_grad[endpoints].astype(jnp.float32)
        edge_sum = jnp.einsum('tek,ted->tkd', gathered.astype(jnp.float32), edge_rows)
        gathered_grad = jnp.einsum('ted,tkd->tek', edge_rows, w_edge.astype(jnp.float32))
        table_grad = jnp.zeros((PINS_DEV + 2 * HALO, D), jnp.float32).at[sources.reshape(-1)].add(gathered_grad.reshape(-1, D))
        local_grad = jnp.dot(preact_grad, w_self.T, preferred_element_type=jnp.float32) + table_grad[:PINS_DEV]
        return (local_grad, table_grad[PINS_DEV:].astype(jnp.bfloat16), self_sum, edge_sum)
    local_grad, halo_grad, self_all, edge_all = lax.map(second_pass, (feats_dev, halos, edge_src, edge_dst, net_rows))
    received = neighbour_rows(halo_grad)
    grad_feats = jax.vmap(lambda local_one, list_one, rec_one: local_one.at[list_one].add(rec_one.astype(jnp.float32)))(local_grad, send_rows, received)
    grad_feats = grad_feats.astype(jnp.bfloat16).reshape(PINS, D)
    grad_scale = 1.0 / math.sqrt(PINS)
    return (predicted.reshape(NETS), grad_feats, lax.optimization_barrier(jnp.sum(self_all, 0)) * grad_scale, lax.optimization_barrier(jnp.sum(edge_all, 0)) * grad_scale, head_total * grad_scale, out_total * grad_scale)
```

```python
import math

import jax
import jax.numpy as jnp
from jax import lax
from jax.sharding import PartitionSpec as P


F32 = jnp.float32
BF16 = jnp.bfloat16


def extended(block, sides, width):
    for axis, dim in sides:
        count = lax.axis_size(axis)
        forward = [(i, i + 1) for i in range(count - 1)]
        backward = [(target, source) for source, target in forward]
        low = lax.ppermute(
            lax.slice_in_dim(block, block.shape[dim] - width, None, axis=dim), axis, forward
        )
        high = lax.ppermute(lax.slice_in_dim(block, 0, width, axis=dim), axis, backward)
        block = jnp.concatenate([low, block, high], axis=dim)
    return block


def silu_slope(values):
    sigma_val = jax.nn.sigmoid(values)
    return sigma_val * (1.0 + values * (1.0 - sigma_val))


def one_hot(index, count):
    return (index[..., None] == jnp.arange(count, dtype=index.dtype)).astype(BF16)


def split_dot(spec, left, right):
    head = left.astype(BF16)
    tail = (left - head.astype(F32)).astype(BF16)
    return jnp.einsum(spec, head, right, preferred_element_type=F32) + jnp.einsum(
        spec, tail, right, preferred_element_type=F32
    )


def on_device(
    pin_feats,
    w_self,
    w_edge,
    w_head,
    w_out,
    send_rows,
    edge_src,
    edge_dst,
    pin_owner,
    pin_net,
    net_target,
):
    pin_count, feat_width = pin_feats.shape
    send_list = send_rows[0]
    halo_span = send_list.shape[0] // 2
    send_hot = one_hot(send_list, pin_count)
    outgoing = jnp.dot(send_hot, pin_feats, preferred_element_type=F32).astype(BF16)
    padded = extended(outgoing, (("dom", 0),), halo_span)
    node_table = jnp.concatenate([pin_feats, padded[:halo_span], padded[3 * halo_span :]], 0)
    table_rows = node_table.shape[0]
    sources = edge_src[0]
    endpoints = edge_dst[0]
    src_hot = one_hot(sources, table_rows)
    dst_hot = one_hot(endpoints, pin_count)
    gathered = jnp.einsum(
        "ter,rd->ted", src_hot, node_table, preferred_element_type=F32
    ).astype(BF16)
    edge_in = jnp.einsum("tep,ted->tpd", dst_hot, gathered, preferred_element_type=F32)
    summed = split_dot("tpk,tkd->pd", edge_in, w_edge)
    degree = jnp.sum(dst_hot.astype(F32), axis=(0, 1))
    inverse = 1.0 / (1.0 + degree)
    preact = (
        jnp.dot(pin_feats, w_self, preferred_element_type=F32) + summed * inverse[:, None]
    )
    hidden = jax.nn.silu(preact).astype(BF16)
    groups = lax.axis_size("group")
    domains = lax.axis_size("dom")
    owners = groups * domains
    capacity = max(2, 2 * pin_count // owners)
    net_count = net_target.shape[0]
    owner_ids = pin_owner[:, 0]
    owner_hot = one_hot(owner_ids, owners)
    earlier = (
        jnp.arange(pin_count, dtype=jnp.int32)[None, :]
        < jnp.arange(pin_count, dtype=jnp.int32)[:, None]
    ).astype(BF16)
    before = jnp.dot(earlier, owner_hot, preferred_element_type=F32)
    slot_rank = jnp.sum(before * owner_hot.astype(F32), axis=1).astype(jnp.int32)
    pin_slot = owner_ids * capacity + slot_rank
    slot_hot = one_hot(pin_slot, owners * capacity)
    net_code = (pin_net + 1).astype(BF16)[:, None]
    slot_nets = (
        jnp.dot(slot_hot.T, net_code, preferred_element_type=F32)[:, 0].astype(jnp.int32) - 1
    )
    slot_nets_in = lax.all_to_all(
        slot_nets.reshape(owners, capacity),
        ("group", "dom"),
        split_axis=0,
        concat_axis=0,
        tiled=True,
    ).reshape(-1)
    outbound = jnp.dot(slot_hot.T, hidden, preferred_element_type=F32).astype(BF16)
    inbound = lax.all_to_all(
        outbound.reshape(owners, capacity, feat_width),
        ("group", "dom"),
        split_axis=0,
        concat_axis=0,
        tiled=True,
    ).reshape(-1, feat_width)
    net_hot = one_hot(slot_nets_in, net_count)
    pooled = jnp.einsum("sn,sd->nd", net_hot, inbound, preferred_element_type=F32)
    pooled_b = pooled.astype(BF16)
    head_pre = jnp.dot(pooled_b, w_head, preferred_element_type=F32)
    activated = jax.nn.silu(head_pre).astype(BF16)
    predicted = jnp.dot(activated, w_out, preferred_element_type=F32)
    misfit = predicted - net_target
    head_grad = (
        misfit[:, None] * w_out.astype(F32)[None, :] * silu_slope(head_pre)
    ).astype(BF16)
    head_sum = jnp.einsum("nd,nh->dh", pooled_b, head_grad, preferred_element_type=F32)
    out_sum = jnp.dot(misfit, activated.astype(F32), precision=lax.Precision.HIGHEST)
    head_totals = lax.psum((head_sum, out_sum), ("group", "dom"))
    net_grad = jnp.einsum(
        "nh,dh->nd", head_grad, w_head, preferred_element_type=F32
    ).astype(BF16)
    returned = jnp.dot(net_hot, net_grad, preferred_element_type=F32).astype(BF16)
    arrived = lax.all_to_all(
        returned.reshape(owners, capacity, feat_width),
        ("group", "dom"),
        split_axis=0,
        concat_axis=0,
        tiled=True,
    ).reshape(-1, feat_width)
    pin_grad = jnp.dot(slot_hot, arrived, preferred_element_type=F32)
    preact_grad = (pin_grad * silu_slope(preact)).astype(BF16)
    self_sum = jnp.einsum("pk,pd->kd", pin_feats, preact_grad, preferred_element_type=F32)
    agg_grad = (preact_grad.astype(F32) * inverse[:, None]).astype(BF16)
    edge_rows = jnp.einsum(
        "tep,pd->ted", dst_hot, agg_grad, preferred_element_type=F32
    ).astype(BF16)
    edge_sum = jnp.einsum("tek,ted->tkd", gathered, edge_rows, preferred_element_type=F32)
    row_in = jnp.einsum("ter,ted->trd", src_hot, edge_rows, preferred_element_type=F32)
    table_grad = split_dot("trd,tkd->rk", row_in, w_edge)
    local_grad = (
        jnp.einsum("pd,kd->pk", preact_grad, w_self, preferred_element_type=F32)
        + table_grad[:pin_count]
    )
    halo_grad = table_grad[pin_count:].astype(BF16)
    back_padded = extended(halo_grad, (("dom", 0),), halo_span)
    received = jnp.concatenate([back_padded[:halo_span], back_padded[3 * halo_span :]], 0)
    grad_feats = (
        local_grad + jnp.einsum("sp,sd->pd", send_hot, received, preferred_element_type=F32)
    ).astype(BF16)
    tail_totals = lax.psum((self_sum, edge_sum), ("group", "dom"))
    grad_scale = 1.0 / math.sqrt(pin_count * owners)
    return (
        predicted,
        grad_feats,
        tail_totals[0] * grad_scale,
        tail_totals[1] * grad_scale,
        head_totals[0] * grad_scale,
        head_totals[1] * grad_scale,
    )


def solution(mesh):
    in_specs = (
        P(("group", "dom"), None),
        P(),
        P(),
        P(),
        P(),
        P(("group", "dom"), None),
        P(("group", "dom"), None, None),
        P(("group", "dom"), None, None),
        P(("group", "dom"), None),
        P(("group", "dom")),
        P(("group", "dom")),
    )
    out_specs = (P(("group", "dom")), P(("group", "dom"), None), P(), P(), P(), P())
    return jax.shard_map(
        on_device, mesh=mesh, in_specs=in_specs, out_specs=out_specs, check_vma=False
    )
```

```python
import math

import jax
import jax.numpy as jnp
from jax import lax
from jax.sharding import PartitionSpec as P


F32 = jnp.float32
BF16 = jnp.bfloat16


def extended(block, sides, width):
    for axis, dim in sides:
        count = lax.axis_size(axis)
        forward = [(i, i + 1) for i in range(count - 1)]
        backward = [(target, source) for source, target in forward]
        low = lax.ppermute(
            lax.slice_in_dim(block, block.shape[dim] - width, None, axis=dim), axis, forward
        )
        high = lax.ppermute(lax.slice_in_dim(block, 0, width, axis=dim), axis, backward)
        block = jnp.concatenate([low, block, high], axis=dim)
    return block


def silu_slope(values):
    sigma_val = jax.nn.sigmoid(values)
    return sigma_val * (1.0 + values * (1.0 - sigma_val))


def one_hot(index, count):
    return (index[..., None] == jnp.arange(count, dtype=index.dtype)).astype(BF16)


def split_dot(spec, left, right):
    return jnp.einsum(
        spec, left, right.astype(F32), precision=lax.Precision.HIGHEST, preferred_element_type=F32
    )


def on_device(
    pin_feats,
    w_self,
    w_edge,
    w_head,
    w_out,
    send_rows,
    edge_src,
    edge_dst,
    pin_owner,
    pin_net,
    net_target,
):
    pin_count, feat_width = pin_feats.shape
    send_list = send_rows[0]
    halo_span = send_list.shape[0] // 2
    send_hot = one_hot(send_list, pin_count)
    outgoing = jnp.dot(send_hot, pin_feats, preferred_element_type=F32).astype(BF16)
    padded = extended(outgoing, (("dom", 0),), halo_span)
    node_table = jnp.concatenate([pin_feats, padded[:halo_span], padded[3 * halo_span :]], 0)
    table_rows = node_table.shape[0]
    sources = edge_src[0]
    endpoints = edge_dst[0]
    src_hot = one_hot(sources, table_rows)
    dst_hot = one_hot(endpoints, pin_count)
    gathered = jnp.einsum(
        "ter,rd->ted", src_hot, node_table, preferred_element_type=F32
    ).astype(BF16)
    edge_in = jnp.einsum("tep,ted->tpd", dst_hot, gathered, preferred_element_type=F32)
    summed = split_dot("tpk,tkd->pd", edge_in, w_edge)
    degree = jnp.sum(dst_hot.astype(F32), axis=(0, 1))
    inverse = 1.0 / (1.0 + degree)
    preact = (
        jnp.dot(pin_feats, w_self, preferred_element_type=F32) + summed * inverse[:, None]
    )
    hidden = jax.nn.silu(preact).astype(BF16)
    groups = lax.axis_size("group")
    domains = lax.axis_size("dom")
    owners = groups * domains
    capacity = max(2, 2 * pin_count // owners)
    net_count = net_target.shape[0]
    owner_ids = pin_owner[:, 0]
    owner_hot = one_hot(owner_ids, owners)
    earlier = (
        jnp.arange(pin_count, dtype=jnp.int32)[None, :]
        < jnp.arange(pin_count, dtype=jnp.int32)[:, None]
    ).astype(BF16)
    before = jnp.dot(earlier, owner_hot, preferred_element_type=F32)
    slot_rank = jnp.sum(before * owner_hot.astype(F32), axis=1).astype(jnp.int32)
    pin_slot = owner_ids * capacity + slot_rank
    slot_hot = one_hot(pin_slot, owners * capacity)
    net_code = (pin_net + 1).astype(BF16)[:, None]
    slot_nets = (
        jnp.dot(slot_hot.T, net_code, preferred_element_type=F32)[:, 0].astype(jnp.int32) - 1
    )
    slot_nets_in = lax.all_to_all(
        slot_nets.reshape(owners, capacity),
        ("group", "dom"),
        split_axis=0,
        concat_axis=0,
        tiled=True,
    ).reshape(-1)
    outbound = jnp.dot(slot_hot.T, hidden, preferred_element_type=F32).astype(BF16)
    inbound = lax.all_to_all(
        outbound.reshape(owners, capacity, feat_width),
        ("group", "dom"),
        split_axis=0,
        concat_axis=0,
        tiled=True,
    ).reshape(-1, feat_width)
    net_hot = one_hot(slot_nets_in, net_count)
    pooled = jnp.einsum("sn,sd->nd", net_hot, inbound, preferred_element_type=F32)
    pooled_b = pooled.astype(BF16)
    head_pre = jnp.dot(pooled_b, w_head, preferred_element_type=F32)
    activated = jax.nn.silu(head_pre).astype(BF16)
    predicted = jnp.dot(activated, w_out, preferred_element_type=F32)
    misfit = predicted - net_target
    head_grad = (
        misfit[:, None] * w_out.astype(F32)[None, :] * silu_slope(head_pre)
    ).astype(BF16)
    head_sum = jnp.einsum("nd,nh->dh", pooled_b, head_grad, preferred_element_type=F32)
    out_sum = jnp.dot(misfit, activated.astype(F32), precision=lax.Precision.HIGHEST)
    head_totals = lax.psum(jnp.concatenate([head_sum, out_sum[None, :]], 0), ("group", "dom"))
    net_grad = jnp.einsum(
        "nh,dh->nd", head_grad, w_head, preferred_element_type=F32
    ).astype(BF16)
    returned = jnp.dot(net_hot, net_grad, preferred_element_type=F32).astype(BF16)
    arrived = lax.all_to_all(
        returned.reshape(owners, capacity, feat_width),
        ("group", "dom"),
        split_axis=0,
        concat_axis=0,
        tiled=True,
    ).reshape(-1, feat_width)
    pin_grad = jnp.dot(slot_hot, arrived, preferred_element_type=F32)
    preact_grad = (pin_grad * silu_slope(preact)).astype(BF16)
    self_sum = jnp.einsum("pk,pd->kd", pin_feats, preact_grad, preferred_element_type=F32)
    agg_grad = (preact_grad.astype(F32) * inverse[:, None]).astype(BF16)
    edge_rows = jnp.einsum(
        "tep,pd->ted", dst_hot, agg_grad, preferred_element_type=F32
    ).astype(BF16)
    edge_sum = jnp.einsum("tek,ted->tkd", gathered, edge_rows, preferred_element_type=F32)
    row_in = jnp.einsum("ter,ted->trd", src_hot, edge_rows, preferred_element_type=F32)
    table_grad = split_dot("trd,tkd->rk", row_in, w_edge)
    local_grad = (
        jnp.einsum("pd,kd->pk", preact_grad, w_self, preferred_element_type=F32)
        + table_grad[:pin_count]
    )
    halo_grad = table_grad[pin_count:].astype(BF16)
    back_padded = extended(halo_grad, (("dom", 0),), halo_span)
    received = jnp.concatenate([back_padded[:halo_span], back_padded[3 * halo_span :]], 0)
    grad_feats = (
        local_grad + jnp.einsum("sp,sd->pd", send_hot, received, preferred_element_type=F32)
    ).astype(BF16)
    self_sum, edge_sum, head_totals = lax.optimization_barrier((self_sum, edge_sum, head_totals))
    tail_totals = lax.psum((self_sum, edge_sum), ("group", "dom"))
    grad_scale = 1.0 / math.sqrt(pin_count * owners)
    return (
        predicted,
        grad_feats,
        tail_totals[0] * grad_scale,
        tail_totals[1] * grad_scale,
        head_totals[:feat_width] * grad_scale,
        head_totals[feat_width] * grad_scale,
    )


def solution(mesh):
    in_specs = (
        P(("group", "dom"), None),
        P(),
        P(),
        P(),
        P(),
        P(("group", "dom"), None),
        P(("group", "dom"), None, None),
        P(("group", "dom"), None, None),
        P(("group", "dom"), None),
        P(("group", "dom")),
        P(("group", "dom")),
    )
    out_specs = (P(("group", "dom")), P(("group", "dom"), None), P(), P(), P(), P())
    return jax.shard_map(
        on_device, mesh=mesh, in_specs=in_specs, out_specs=out_specs, check_vma=False
    )
```

```python
import math

import jax
import jax.numpy as jnp
from jax import lax
from jax.sharding import PartitionSpec as P


F32 = jnp.float32
BF16 = jnp.bfloat16


def extended(block, sides, width):
    for axis, dim in sides:
        count = lax.axis_size(axis)
        forward = [(i, i + 1) for i in range(count - 1)]
        backward = [(target, source) for source, target in forward]
        low = lax.ppermute(
            lax.slice_in_dim(block, block.shape[dim] - width, None, axis=dim), axis, forward
        )
        high = lax.ppermute(lax.slice_in_dim(block, 0, width, axis=dim), axis, backward)
        block = jnp.concatenate([low, block, high], axis=dim)
    return block


def silu_slope(values):
    sigma_val = jax.nn.sigmoid(values)
    return sigma_val * (1.0 + values * (1.0 - sigma_val))


def one_hot(index, count):
    return (index[..., None] == jnp.arange(count, dtype=index.dtype)).astype(BF16)


def split_dot(spec, left, right):
    return jnp.einsum(
        spec, left, right.astype(F32), precision=lax.Precision.HIGHEST, preferred_element_type=F32
    )


def all_sum(parts, owners):
    flat = jnp.concatenate(parts)
    unit = owners * 128
    length = -(-flat.shape[0] // unit) * unit
    flat = jnp.pad(flat, (0, length - flat.shape[0]))
    axes = ("group", "dom")
    mine = lax.all_to_all(
        flat.astype(BF16).reshape(owners, -1), axes, split_axis=0, concat_axis=0, tiled=True
    )
    mine = jnp.sum(mine.astype(F32), axis=0).astype(BF16)
    spread = jnp.broadcast_to(mine[None], (owners, mine.shape[0]))
    gathered = lax.all_to_all(spread, axes, split_axis=0, concat_axis=0, tiled=True)
    return gathered.astype(F32).reshape(-1)


def on_device(
    pin_feats,
    w_self,
    w_edge,
    w_head,
    w_out,
    send_rows,
    edge_src,
    edge_dst,
    pin_owner,
    pin_net,
    net_target,
):
    pin_count, feat_width = pin_feats.shape
    send_list = send_rows[0]
    halo_span = send_list.shape[0] // 2
    send_hot = one_hot(send_list, pin_count)
    outgoing = jnp.dot(send_hot, pin_feats, preferred_element_type=F32).astype(BF16)
    padded = extended(outgoing, (("dom", 0),), halo_span)
    node_table = jnp.concatenate([pin_feats, padded[:halo_span], padded[3 * halo_span :]], 0)
    table_rows = node_table.shape[0]
    sources = edge_src[0]
    endpoints = edge_dst[0]
    src_hot = one_hot(sources, table_rows)
    dst_hot = one_hot(endpoints, pin_count)
    gathered = jnp.einsum(
        "ter,rd->ted", src_hot, node_table, preferred_element_type=F32
    ).astype(BF16)
    edge_in = jnp.einsum("tep,ted->tpd", dst_hot, gathered, preferred_element_type=F32)
    summed = split_dot("tpk,tkd->pd", edge_in, w_edge)
    degree = jnp.sum(dst_hot.astype(F32), axis=(0, 1))
    inverse = 1.0 / (1.0 + degree)
    preact = (
        jnp.dot(pin_feats, w_self, preferred_element_type=F32) + summed * inverse[:, None]
    )
    hidden = jax.nn.silu(preact).astype(BF16)
    groups = lax.axis_size("group")
    domains = lax.axis_size("dom")
    owners = groups * domains
    capacity = max(2, 2 * pin_count // owners)
    net_count = net_target.shape[0]
    owner_ids = pin_owner[:, 0]
    owner_hot = one_hot(owner_ids, owners)
    earlier = (
        jnp.arange(pin_count, dtype=jnp.int32)[None, :]
        < jnp.arange(pin_count, dtype=jnp.int32)[:, None]
    ).astype(BF16)
    before = jnp.dot(earlier, owner_hot, preferred_element_type=F32)
    slot_rank = jnp.sum(before * owner_hot.astype(F32), axis=1).astype(jnp.int32)
    pin_slot = owner_ids * capacity + slot_rank
    slot_hot = one_hot(pin_slot, owners * capacity)
    net_code = (pin_net + 1).astype(BF16)[:, None]
    slot_nets = jnp.dot(slot_hot.T, net_code, preferred_element_type=F32)[:, 0] - 1.0
    outbound = jnp.dot(slot_hot.T, hidden, preferred_element_type=F32).astype(BF16)
    id_rows = -(-capacity // feat_width)
    id_block = jnp.pad(
        slot_nets.reshape(owners, capacity), ((0, 0), (0, id_rows * feat_width - capacity))
    ).astype(BF16)
    packet = jnp.concatenate(
        [
            outbound.reshape(owners, capacity, feat_width),
            id_block.reshape(owners, id_rows, feat_width),
        ],
        1,
    )
    packet_in = lax.all_to_all(packet, ("group", "dom"), split_axis=0, concat_axis=0, tiled=True)
    inbound = packet_in[:, :capacity].reshape(-1, feat_width)
    slot_nets_in = (
        packet_in[:, capacity:].reshape(owners, -1)[:, :capacity].astype(F32).astype(jnp.int32)
    ).reshape(-1)
    net_hot = one_hot(slot_nets_in, net_count)
    pooled = jnp.einsum("sn,sd->nd", net_hot, inbound, preferred_element_type=F32)
    pooled_b = pooled.astype(BF16)
    head_pre = jnp.dot(pooled_b, w_head, preferred_element_type=F32)
    activated = jax.nn.silu(head_pre).astype(BF16)
    predicted = jnp.dot(activated, w_out, preferred_element_type=F32)
    misfit = predicted - net_target
    head_grad = (
        misfit[:, None] * w_out.astype(F32)[None, :] * silu_slope(head_pre)
    ).astype(BF16)
    head_sum = jnp.einsum("nd,nh->dh", pooled_b, head_grad, preferred_element_type=F32)
    out_sum = jnp.dot(misfit, activated.astype(F32), precision=lax.Precision.HIGHEST)
    net_grad = jnp.einsum(
        "nh,dh->nd", head_grad, w_head, preferred_element_type=F32
    ).astype(BF16)
    returned = jnp.dot(net_hot, net_grad, preferred_element_type=F32).astype(BF16)
    arrived = lax.all_to_all(
        returned.reshape(owners, capacity, feat_width),
        ("group", "dom"),
        split_axis=0,
        concat_axis=0,
        tiled=True,
    ).reshape(-1, feat_width)
    pin_grad = jnp.dot(slot_hot, arrived, preferred_element_type=F32)
    preact_grad = (pin_grad * silu_slope(preact)).astype(BF16)
    self_sum = jnp.einsum("pk,pd->kd", pin_feats, preact_grad, preferred_element_type=F32)
    agg_grad = (preact_grad.astype(F32) * inverse[:, None]).astype(BF16)
    edge_rows = jnp.einsum(
        "tep,pd->ted", dst_hot, agg_grad, preferred_element_type=F32
    ).astype(BF16)
    edge_sum = jnp.einsum("tek,ted->tkd", gathered, edge_rows, preferred_element_type=F32)
    row_in = jnp.einsum("ter,ted->trd", src_hot, edge_rows, preferred_element_type=F32)
    table_grad = split_dot("trd,tkd->rk", row_in, w_edge)
    local_grad = (
        jnp.einsum("pd,kd->pk", preact_grad, w_self, preferred_element_type=F32)
        + table_grad[:pin_count]
    )
    halo_grad = table_grad[pin_count:].astype(BF16)
    back_padded = extended(halo_grad, (("dom", 0),), halo_span)
    received = jnp.concatenate([back_padded[:halo_span], back_padded[3 * halo_span :]], 0)
    grad_feats = (
        local_grad + jnp.einsum("sp,sd->pd", send_hot, received, preferred_element_type=F32)
    ).astype(BF16)
    pieces = (self_sum, edge_sum, head_sum, out_sum)
    totals = all_sum([piece.reshape(-1) for piece in pieces], owners)
    grad_scale = 1.0 / math.sqrt(pin_count * owners)
    outs = []
    offset = 0
    for piece in pieces:
        outs.append(totals[offset : offset + piece.size].reshape(piece.shape) * grad_scale)
        offset += piece.size
    return (predicted, grad_feats, outs[0], outs[1], outs[2], outs[3])


def solution(mesh):
    in_specs = (
        P(("group", "dom"), None),
        P(),
        P(),
        P(),
        P(),
        P(("group", "dom"), None),
        P(("group", "dom"), None, None),
        P(("group", "dom"), None, None),
        P(("group", "dom"), None),
        P(("group", "dom")),
        P(("group", "dom")),
    )
    out_specs = (P(("group", "dom")), P(("group", "dom"), None), P(), P(), P(), P())
    return jax.shard_map(
        on_device, mesh=mesh, in_specs=in_specs, out_specs=out_specs, check_vma=False
    )
```

```python
import math

import jax
import jax.numpy as jnp
from jax import lax
from jax.sharding import PartitionSpec as P


F32 = jnp.float32
BF16 = jnp.bfloat16


def extended(block, sides, width):
    for axis, dim in sides:
        count = lax.axis_size(axis)
        forward = [(i, i + 1) for i in range(count - 1)]
        backward = [(target, source) for source, target in forward]
        low = lax.ppermute(
            lax.slice_in_dim(block, block.shape[dim] - width, None, axis=dim), axis, forward
        )
        high = lax.ppermute(lax.slice_in_dim(block, 0, width, axis=dim), axis, backward)
        block = jnp.concatenate([low, block, high], axis=dim)
    return block


def silu_slope(values):
    sigma_val = jax.nn.sigmoid(values)
    return sigma_val * (1.0 + values * (1.0 - sigma_val))


def one_hot(index, count):
    return (index[..., None] == jnp.arange(count, dtype=index.dtype)).astype(BF16)


def split_dot(spec, left, right):
    return jnp.einsum(
        spec, left, right.astype(F32), precision=lax.Precision.HIGHEST, preferred_element_type=F32
    )


def all_sum(rows, owners):
    count, width = rows.shape
    unit = owners * 16
    length = -(-count // unit) * unit
    rows = jnp.pad(rows, ((0, length - count), (0, 0)))
    axes = ("group", "dom")
    mine = lax.all_to_all(
        rows.astype(BF16).reshape(owners, -1, width), axes, split_axis=0, concat_axis=0, tiled=True
    )
    mine = jnp.sum(mine.astype(F32), axis=0).astype(BF16)
    spread = jnp.broadcast_to(mine[None], (owners,) + mine.shape)
    gathered = lax.all_to_all(spread, axes, split_axis=0, concat_axis=0, tiled=True)
    return gathered.reshape(length, width)[:count].astype(F32)


def on_device(
    pin_feats,
    w_self,
    w_edge,
    w_head,
    w_out,
    send_rows,
    edge_src,
    edge_dst,
    pin_owner,
    pin_net,
    net_target,
):
    pin_count, feat_width = pin_feats.shape
    send_list = send_rows[0]
    halo_span = send_list.shape[0] // 2
    send_hot = one_hot(send_list, pin_count)
    outgoing = jnp.dot(send_hot, pin_feats, preferred_element_type=F32).astype(BF16)
    padded = extended(outgoing, (("dom", 0),), halo_span)
    node_table = jnp.concatenate([pin_feats, padded[:halo_span], padded[3 * halo_span :]], 0)
    table_rows = node_table.shape[0]
    sources = edge_src[0]
    endpoints = edge_dst[0]
    src_hot = one_hot(sources, table_rows)
    dst_hot = one_hot(endpoints, pin_count)
    gathered = jnp.einsum(
        "ter,rd->ted", src_hot, node_table, preferred_element_type=F32
    ).astype(BF16)
    edge_in = jnp.einsum("tep,ted->tpd", dst_hot, gathered, preferred_element_type=F32)
    summed = split_dot("tpk,tkd->pd", edge_in, w_edge)
    degree = jnp.sum(dst_hot.astype(F32), axis=(0, 1))
    inverse = 1.0 / (1.0 + degree)
    preact = (
        jnp.dot(pin_feats, w_self, preferred_element_type=F32) + summed * inverse[:, None]
    )
    hidden = jax.nn.silu(preact).astype(BF16)
    groups = lax.axis_size("group")
    domains = lax.axis_size("dom")
    owners = groups * domains
    capacity = max(2, 2 * pin_count // owners)
    net_count = net_target.shape[0]
    owner_ids = pin_owner[:, 0]
    owner_hot = one_hot(owner_ids, owners)
    earlier = (
        jnp.arange(pin_count, dtype=jnp.int32)[None, :]
        < jnp.arange(pin_count, dtype=jnp.int32)[:, None]
    ).astype(BF16)
    before = jnp.dot(earlier, owner_hot, preferred_element_type=F32)
    slot_rank = jnp.sum(before * owner_hot.astype(F32), axis=1).astype(jnp.int32)
    pin_slot = owner_ids * capacity + slot_rank
    slot_hot = one_hot(pin_slot, owners * capacity)
    net_code = (pin_net + 1).astype(BF16)[:, None]
    slot_nets = jnp.dot(slot_hot.T, net_code, preferred_element_type=F32)[:, 0] - 1.0
    outbound = jnp.dot(slot_hot.T, hidden, preferred_element_type=F32).astype(BF16)
    id_rows = -(-capacity // feat_width)
    id_block = jnp.pad(
        slot_nets.reshape(owners, capacity), ((0, 0), (0, id_rows * feat_width - capacity))
    ).astype(BF16)
    packet = jnp.concatenate(
        [
            outbound.reshape(owners, capacity, feat_width),
            id_block.reshape(owners, id_rows, feat_width),
        ],
        1,
    )
    packet_in = lax.all_to_all(packet, ("group", "dom"), split_axis=0, concat_axis=0, tiled=True)
    inbound = packet_in[:, :capacity].reshape(-1, feat_width)
    slot_nets_in = (
        packet_in[:, capacity:].reshape(owners, -1)[:, :capacity].astype(F32).astype(jnp.int32)
    ).reshape(-1)
    net_hot = one_hot(slot_nets_in, net_count)
    pooled = jnp.einsum("sn,sd->nd", net_hot, inbound, preferred_element_type=F32)
    pooled_b = pooled.astype(BF16)
    head_pre = jnp.dot(pooled_b, w_head, preferred_element_type=F32)
    activated = jax.nn.silu(head_pre).astype(BF16)
    predicted = jnp.dot(activated, w_out, preferred_element_type=F32)
    misfit = predicted - net_target
    head_grad = (
        misfit[:, None] * w_out.astype(F32)[None, :] * silu_slope(head_pre)
    ).astype(BF16)
    head_sum_t = jnp.einsum("nh,nd->hd", head_grad, pooled_b, preferred_element_type=F32)
    out_sum = jnp.dot(misfit, activated.astype(F32), precision=lax.Precision.HIGHEST)
    net_grad = jnp.einsum(
        "nh,dh->nd", head_grad, w_head, preferred_element_type=F32
    ).astype(BF16)
    returned = jnp.dot(net_hot, net_grad, preferred_element_type=F32).astype(BF16)
    arrived = lax.all_to_all(
        returned.reshape(owners, capacity, feat_width),
        ("group", "dom"),
        split_axis=0,
        concat_axis=0,
        tiled=True,
    ).reshape(-1, feat_width)
    pin_grad = jnp.dot(slot_hot, arrived, preferred_element_type=F32)
    preact_grad = (pin_grad * silu_slope(preact)).astype(BF16)
    self_sum = jnp.einsum("pk,pd->kd", pin_feats, preact_grad, preferred_element_type=F32)
    agg_grad = (preact_grad.astype(F32) * inverse[:, None]).astype(BF16)
    edge_rows = jnp.einsum(
        "tep,pd->ted", dst_hot, agg_grad, preferred_element_type=F32
    ).astype(BF16)
    edge_sum = jnp.einsum("tek,ted->tkd", gathered, edge_rows, preferred_element_type=F32)
    row_in = jnp.einsum("ter,ted->trd", src_hot, edge_rows, preferred_element_type=F32)
    table_grad = split_dot("trd,tkd->rk", row_in, w_edge)
    local_grad = (
        jnp.einsum("pd,kd->pk", preact_grad, w_self, preferred_element_type=F32)
        + table_grad[:pin_count]
    )
    halo_grad = table_grad[pin_count:].astype(BF16)
    back_padded = extended(halo_grad, (("dom", 0),), halo_span)
    received = jnp.concatenate([back_padded[:halo_span], back_padded[3 * halo_span :]], 0)
    grad_feats = (
        local_grad + jnp.einsum("sp,sd->pd", send_hot, received, preferred_element_type=F32)
    ).astype(BF16)
    head_width = head_sum_t.shape[0]
    pieces = (
        self_sum,
        edge_sum.reshape(-1, feat_width),
        head_sum_t,
        out_sum.reshape(-1, feat_width),
    )
    totals = all_sum(jnp.concatenate(pieces, 0), owners)
    grad_scale = 1.0 / math.sqrt(pin_count * owners)
    outs = []
    offset = 0
    for piece in pieces:
        outs.append(totals[offset : offset + piece.shape[0]] * grad_scale)
        offset += piece.shape[0]
    return (
        predicted,
        grad_feats,
        outs[0],
        outs[1].reshape(edge_sum.shape),
        outs[2].T,
        outs[3].reshape(head_width),
    )


def solution(mesh):
    in_specs = (
        P(("group", "dom"), None),
        P(),
        P(),
        P(),
        P(),
        P(("group", "dom"), None),
        P(("group", "dom"), None, None),
        P(("group", "dom"), None, None),
        P(("group", "dom"), None),
        P(("group", "dom")),
        P(("group", "dom")),
    )
    out_specs = (P(("group", "dom")), P(("group", "dom"), None), P(), P(), P(), P())
    return jax.shard_map(
        on_device, mesh=mesh, in_specs=in_specs, out_specs=out_specs, check_vma=False
    )
```

```python
import math

import jax
import jax.numpy as jnp
from jax import lax
from jax.sharding import PartitionSpec as P


F32 = jnp.float32
BF16 = jnp.bfloat16


def extended(block, sides, width):
    for axis, dim in sides:
        count = lax.axis_size(axis)
        forward = [(i, i + 1) for i in range(count - 1)]
        backward = [(target, source) for source, target in forward]
        low = lax.ppermute(
            lax.slice_in_dim(block, block.shape[dim] - width, None, axis=dim), axis, forward
        )
        high = lax.ppermute(lax.slice_in_dim(block, 0, width, axis=dim), axis, backward)
        block = jnp.concatenate([low, block, high], axis=dim)
    return block


def silu_slope(values):
    sigma_val = jax.nn.sigmoid(values)
    return sigma_val * (1.0 + values * (1.0 - sigma_val))


def one_hot(index, count):
    return (index[..., None] == jnp.arange(count, dtype=index.dtype)).astype(BF16)


def split_dot(spec, left, right):
    return jnp.einsum(
        spec, left, right.astype(F32), precision=lax.Precision.HIGHEST, preferred_element_type=F32
    )


def all_sum(rows, owners):
    count, width = rows.shape
    unit = owners * 16
    length = -(-count // unit) * unit
    rows = jnp.pad(rows, ((0, length - count), (0, 0)))
    axes = ("group", "dom")
    mine = lax.all_to_all(
        rows.astype(BF16).reshape(owners, -1, width), axes, split_axis=0, concat_axis=0, tiled=True
    )
    mine = jnp.einsum(
        "o,orw->rw", jnp.ones((owners,), BF16), mine, preferred_element_type=F32
    ).astype(BF16)
    spread = jnp.broadcast_to(mine[None], (owners,) + mine.shape)
    gathered = lax.all_to_all(spread, axes, split_axis=0, concat_axis=0, tiled=True)
    return gathered.reshape(length, width)[:count].astype(F32)


def on_device(
    pin_feats,
    w_self,
    w_edge,
    w_head,
    w_out,
    send_rows,
    edge_src,
    edge_dst,
    pin_owner,
    pin_net,
    net_target,
):
    pin_count, feat_width = pin_feats.shape
    send_list = send_rows[0]
    halo_span = send_list.shape[0] // 2
    send_hot = one_hot(send_list, pin_count)
    outgoing = jnp.dot(send_hot, pin_feats, preferred_element_type=F32).astype(BF16)
    padded = extended(outgoing, (("dom", 0),), halo_span)
    node_table = jnp.concatenate([pin_feats, padded[:halo_span], padded[3 * halo_span :]], 0)
    table_rows = node_table.shape[0]
    sources = edge_src[0]
    endpoints = edge_dst[0]
    src_hot = one_hot(sources, table_rows)
    dst_hot = one_hot(endpoints, pin_count)
    gathered = jnp.einsum(
        "ter,rd->ted", src_hot, node_table, preferred_element_type=F32
    ).astype(BF16)
    edge_in = jnp.einsum("tep,ted->tpd", dst_hot, gathered, preferred_element_type=F32)
    summed = split_dot("tpk,tkd->pd", edge_in, w_edge)
    degree = jnp.sum(dst_hot.astype(F32), axis=(0, 1))
    inverse = 1.0 / (1.0 + degree)
    preact = (
        jnp.dot(pin_feats, w_self, preferred_element_type=F32) + summed * inverse[:, None]
    )
    hidden = jax.nn.silu(preact).astype(BF16)
    groups = lax.axis_size("group")
    domains = lax.axis_size("dom")
    owners = groups * domains
    capacity = max(2, 2 * pin_count // owners)
    net_count = net_target.shape[0]
    owner_ids = pin_owner[:, 0]
    owner_hot = one_hot(owner_ids, owners)
    earlier = (
        jnp.arange(pin_count, dtype=jnp.int32)[None, :]
        < jnp.arange(pin_count, dtype=jnp.int32)[:, None]
    ).astype(BF16)
    before = jnp.dot(earlier, owner_hot, preferred_element_type=F32)
    slot_rank = jnp.sum(before * owner_hot.astype(F32), axis=1).astype(jnp.int32)
    pin_slot = owner_ids * capacity + slot_rank
    slot_hot = one_hot(pin_slot, owners * capacity)
    net_code = (pin_net + 1).astype(BF16)[:, None]
    slot_nets = jnp.dot(slot_hot.T, net_code, preferred_element_type=F32)[:, 0] - 1.0
    outbound = jnp.dot(slot_hot.T, hidden, preferred_element_type=F32).astype(BF16)
    id_rows = -(-capacity // feat_width)
    id_block = jnp.pad(
        slot_nets.reshape(owners, capacity), ((0, 0), (0, id_rows * feat_width - capacity))
    ).astype(BF16)
    packet = jnp.concatenate(
        [
            outbound.reshape(owners, capacity, feat_width),
            id_block.reshape(owners, id_rows, feat_width),
        ],
        1,
    )
    packet_in = lax.all_to_all(packet, ("group", "dom"), split_axis=0, concat_axis=0, tiled=True)
    inbound = packet_in[:, :capacity].reshape(-1, feat_width)
    slot_nets_in = (
        packet_in[:, capacity:].reshape(owners, -1)[:, :capacity].astype(F32).astype(jnp.int32)
    ).reshape(-1)
    net_hot = one_hot(slot_nets_in, net_count)
    pooled = jnp.einsum("sn,sd->nd", net_hot, inbound, preferred_element_type=F32)
    pooled_b = pooled.astype(BF16)
    head_pre = jnp.dot(pooled_b, w_head, preferred_element_type=F32)
    activated = jax.nn.silu(head_pre).astype(BF16)
    predicted = jnp.dot(activated, w_out, preferred_element_type=F32)
    misfit = predicted - net_target
    head_grad = (
        misfit[:, None] * w_out.astype(F32)[None, :] * silu_slope(head_pre)
    ).astype(BF16)
    head_sum_t = jnp.einsum("nh,nd->hd", head_grad, pooled_b, preferred_element_type=F32)
    out_sum = jnp.dot(misfit, activated.astype(F32), precision=lax.Precision.HIGHEST)
    head_width = head_sum_t.shape[0]
    head_totals = all_sum(
        jnp.concatenate([head_sum_t, out_sum.reshape(-1, feat_width)], 0), owners
    )
    net_grad = jnp.einsum(
        "nh,dh->nd", head_grad, w_head, preferred_element_type=F32
    ).astype(BF16)
    returned = jnp.dot(net_hot, net_grad, preferred_element_type=F32).astype(BF16)
    arrived = lax.all_to_all(
        returned.reshape(owners, capacity, feat_width),
        ("group", "dom"),
        split_axis=0,
        concat_axis=0,
        tiled=True,
    ).reshape(-1, feat_width)
    pin_grad = jnp.dot(slot_hot, arrived, preferred_element_type=F32)
    preact_grad = (pin_grad * silu_slope(preact)).astype(BF16)
    self_sum = jnp.einsum("pk,pd->kd", pin_feats, preact_grad, preferred_element_type=F32)
    agg_grad = (preact_grad.astype(F32) * inverse[:, None]).astype(BF16)
    edge_rows = jnp.einsum(
        "tep,pd->ted", dst_hot, agg_grad, preferred_element_type=F32
    ).astype(BF16)
    edge_sum = jnp.einsum("tek,ted->tkd", gathered, edge_rows, preferred_element_type=F32)
    row_in = jnp.einsum("ter,ted->trd", src_hot, edge_rows, preferred_element_type=F32)
    table_grad = split_dot("trd,tkd->rk", row_in, w_edge)
    local_grad = (
        jnp.einsum("pd,kd->pk", preact_grad, w_self, preferred_element_type=F32)
        + table_grad[:pin_count]
    )
    halo_grad = table_grad[pin_count:].astype(BF16)
    back_padded = extended(halo_grad, (("dom", 0),), halo_span)
    received = jnp.concatenate([back_padded[:halo_span], back_padded[3 * halo_span :]], 0)
    grad_feats = (
        local_grad + jnp.einsum("sp,sd->pd", send_hot, received, preferred_element_type=F32)
    ).astype(BF16)
    tail_totals = all_sum(jnp.concatenate([self_sum, edge_sum.reshape(-1, feat_width)], 0), owners)
    grad_scale = 1.0 / math.sqrt(pin_count * owners)
    return (
        predicted,
        grad_feats,
        tail_totals[:feat_width] * grad_scale,
        tail_totals[feat_width:].reshape(edge_sum.shape) * grad_scale,
        head_totals[:head_width].T * grad_scale,
        head_totals[head_width:].reshape(head_width) * grad_scale,
    )


def solution(mesh):
    in_specs = (
        P(("group", "dom"), None),
        P(),
        P(),
        P(),
        P(),
        P(("group", "dom"), None),
        P(("group", "dom"), None, None),
        P(("group", "dom"), None, None),
        P(("group", "dom"), None),
        P(("group", "dom")),
        P(("group", "dom")),
    )
    out_specs = (P(("group", "dom")), P(("group", "dom"), None), P(), P(), P(), P())
    return jax.shard_map(
        on_device, mesh=mesh, in_specs=in_specs, out_specs=out_specs, check_vma=False
    )
```

```python
import math

import jax
import jax.numpy as jnp
from jax import lax
from jax.sharding import PartitionSpec as P


F32 = jnp.float32
BF16 = jnp.bfloat16


def extended(block, sides, width):
    for axis, dim in sides:
        count = lax.axis_size(axis)
        forward = [(i, i + 1) for i in range(count - 1)]
        backward = [(target, source) for source, target in forward]
        low = lax.ppermute(
            lax.slice_in_dim(block, block.shape[dim] - width, None, axis=dim), axis, forward
        )
        high = lax.ppermute(lax.slice_in_dim(block, 0, width, axis=dim), axis, backward)
        block = jnp.concatenate([low, block, high], axis=dim)
    return block


def silu_slope(values):
    sigma_val = jax.nn.sigmoid(values)
    return sigma_val * (1.0 + values * (1.0 - sigma_val))


def one_hot(index, count):
    return (index[..., None] == jnp.arange(count, dtype=index.dtype)).astype(BF16)


def split_dot(spec, left, right):
    return jnp.einsum(
        spec, left, right.astype(F32), precision=lax.Precision.HIGHEST, preferred_element_type=F32
    )


def all_sum(rows, owners):
    count, width = rows.shape
    unit = owners * 16
    length = -(-count // unit) * unit
    rows = jnp.pad(rows, ((0, length - count), (0, 0)))
    axes = ("group", "dom")
    mine = lax.all_to_all(
        rows.astype(BF16).reshape(owners, -1, width), axes, split_axis=0, concat_axis=0, tiled=True
    )
    mine = jnp.einsum(
        "o,orw->rw", jnp.ones((owners,), BF16), mine, preferred_element_type=F32
    ).astype(BF16)
    spread = jnp.broadcast_to(mine[None], (owners,) + mine.shape)
    gathered = lax.all_to_all(spread, axes, split_axis=0, concat_axis=0, tiled=True)
    return gathered.reshape(length, width)[:count].astype(F32)


def on_device(
    pin_feats,
    w_self,
    w_edge,
    w_head,
    w_out,
    send_rows,
    edge_src,
    edge_dst,
    pin_owner,
    pin_net,
    net_target,
):
    pin_count, feat_width = pin_feats.shape
    send_list = send_rows[0]
    halo_span = send_list.shape[0] // 2
    send_hot = one_hot(send_list, pin_count)
    outgoing = jnp.dot(send_hot, pin_feats, preferred_element_type=F32).astype(BF16)
    padded = extended(outgoing, (("dom", 0),), halo_span)
    node_table = jnp.concatenate([pin_feats, padded[:halo_span], padded[3 * halo_span :]], 0)
    table_rows = node_table.shape[0]
    sources = edge_src[0]
    endpoints = edge_dst[0]
    src_hot = one_hot(sources, table_rows)
    dst_hot = one_hot(endpoints, pin_count)
    gathered = jnp.einsum(
        "ter,rd->ted", src_hot, node_table, preferred_element_type=F32
    ).astype(BF16)
    edge_in = jnp.einsum("tep,ted->tpd", dst_hot, gathered, preferred_element_type=F32)
    summed = split_dot("tpk,tkd->pd", edge_in, w_edge)
    degree = jnp.sum(dst_hot.astype(F32), axis=(0, 1))
    inverse = 1.0 / (1.0 + degree)
    preact = (
        jnp.dot(pin_feats, w_self, preferred_element_type=F32) + summed * inverse[:, None]
    )
    hidden = jax.nn.silu(preact).astype(BF16)
    groups = lax.axis_size("group")
    domains = lax.axis_size("dom")
    owners = groups * domains
    capacity = max(2, 2 * pin_count // owners)
    net_count = net_target.shape[0]
    owner_ids = pin_owner[:, 0]
    owner_hot = one_hot(owner_ids, owners)
    earlier = (
        jnp.arange(pin_count, dtype=jnp.int32)[None, :]
        < jnp.arange(pin_count, dtype=jnp.int32)[:, None]
    ).astype(BF16)
    before = jnp.dot(earlier, owner_hot, preferred_element_type=F32)
    slot_rank = jnp.sum(before * owner_hot.astype(F32), axis=1).astype(jnp.int32)
    pin_slot = owner_ids * capacity + slot_rank
    slot_hot = one_hot(pin_slot, owners * capacity)
    net_code = (pin_net + 1).astype(BF16)[:, None]
    slot_nets = jnp.dot(slot_hot.T, net_code, preferred_element_type=F32)[:, 0] - 1.0
    outbound = jnp.dot(slot_hot.T, hidden, preferred_element_type=F32).astype(BF16)
    id_rows = -(-capacity // feat_width)
    id_block = jnp.pad(
        slot_nets.reshape(owners, capacity), ((0, 0), (0, id_rows * feat_width - capacity))
    ).astype(BF16)
    packet = jnp.concatenate(
        [
            outbound.reshape(owners, capacity, feat_width),
            id_block.reshape(owners, id_rows, feat_width),
        ],
        1,
    )
    packet_in = lax.all_to_all(packet, ("group", "dom"), split_axis=0, concat_axis=0, tiled=True)
    inbound = packet_in[:, :capacity].reshape(-1, feat_width)
    slot_nets_in = (
        packet_in[:, capacity:].reshape(owners, -1)[:, :capacity].astype(F32).astype(jnp.int32)
    ).reshape(-1)
    net_hot = one_hot(slot_nets_in, net_count)
    pooled = jnp.einsum("sn,sd->nd", net_hot, inbound, preferred_element_type=F32)
    pooled_b = pooled.astype(BF16)
    head_pre = jnp.dot(pooled_b, w_head, preferred_element_type=F32)
    activated = jax.nn.silu(head_pre).astype(BF16)
    predicted = jnp.dot(activated, w_out, preferred_element_type=F32)
    misfit = predicted - net_target
    head_grad = (
        misfit[:, None] * w_out.astype(F32)[None, :] * silu_slope(head_pre)
    ).astype(BF16)
    head_sum_t = jnp.einsum("nh,nd->hd", head_grad, pooled_b, preferred_element_type=F32)
    out_sum = jnp.dot(misfit, activated.astype(F32), precision=lax.Precision.HIGHEST)
    net_grad = jnp.einsum(
        "nh,dh->nd", head_grad, w_head, preferred_element_type=F32
    ).astype(BF16)
    returned = jnp.dot(net_hot, net_grad, preferred_element_type=F32).astype(BF16)
    arrived = lax.all_to_all(
        returned.reshape(owners, capacity, feat_width),
        ("group", "dom"),
        split_axis=0,
        concat_axis=0,
        tiled=True,
    ).reshape(-1, feat_width)
    pin_grad = jnp.dot(slot_hot, arrived, preferred_element_type=F32)
    preact_grad = (pin_grad * silu_slope(preact)).astype(BF16)
    self_sum = jnp.einsum("pk,pd->kd", pin_feats, preact_grad, preferred_element_type=F32)
    agg_grad = (preact_grad.astype(F32) * inverse[:, None]).astype(BF16)
    edge_rows = jnp.einsum(
        "tep,pd->ted", dst_hot, agg_grad, preferred_element_type=F32
    ).astype(BF16)
    edge_sum = jnp.einsum("tek,ted->tkd", gathered, edge_rows, preferred_element_type=F32)
    row_in = jnp.einsum("ter,ted->trd", src_hot, edge_rows, preferred_element_type=F32)
    table_grad = split_dot("trd,tkd->rk", row_in, w_edge)
    local_grad = (
        jnp.einsum("pd,kd->pk", preact_grad, w_self, preferred_element_type=F32)
        + table_grad[:pin_count]
    )
    halo_grad = table_grad[pin_count:].astype(BF16)
    back_padded = extended(halo_grad, (("dom", 0),), halo_span)
    received = jnp.concatenate([back_padded[:halo_span], back_padded[3 * halo_span :]], 0)
    grad_feats = (
        local_grad + jnp.einsum("sp,sd->pd", send_hot, received, preferred_element_type=F32)
    ).astype(BF16)
    head_width = head_sum_t.shape[0]
    pieces = (
        self_sum,
        edge_sum.reshape(-1, feat_width),
        head_sum_t,
        out_sum.reshape(-1, feat_width),
    )
    totals = all_sum(jnp.concatenate(pieces, 0), owners)
    grad_scale = 1.0 / math.sqrt(pin_count * owners)
    outs = []
    offset = 0
    for piece in pieces:
        outs.append(totals[offset : offset + piece.shape[0]] * grad_scale)
        offset += piece.shape[0]
    return (
        predicted,
        grad_feats,
        outs[0],
        outs[1].reshape(edge_sum.shape),
        outs[2].T,
        outs[3].reshape(head_width),
    )


def solution(mesh):
    in_specs = (
        P(("group", "dom"), None),
        P(),
        P(),
        P(),
        P(),
        P(("group", "dom"), None),
        P(("group", "dom"), None, None),
        P(("group", "dom"), None, None),
        P(("group", "dom"), None),
        P(("group", "dom")),
        P(("group", "dom")),
    )
    out_specs = (P(("group", "dom")), P(("group", "dom"), None), P(), P(), P(), P())
    return jax.shard_map(
        on_device, mesh=mesh, in_specs=in_specs, out_specs=out_specs, check_vma=False
    )
```

```python
import math

import jax
import jax.numpy as jnp
from jax import lax
from jax.sharding import PartitionSpec as P


F32 = jnp.float32
BF16 = jnp.bfloat16


def extended(block, sides, width):
    for axis, dim in sides:
        count = lax.axis_size(axis)
        forward = [(i, i + 1) for i in range(count - 1)]
        backward = [(target, source) for source, target in forward]
        low = lax.ppermute(
            lax.slice_in_dim(block, block.shape[dim] - width, None, axis=dim), axis, forward
        )
        high = lax.ppermute(lax.slice_in_dim(block, 0, width, axis=dim), axis, backward)
        block = jnp.concatenate([low, block, high], axis=dim)
    return block


def silu_slope(values):
    sigma_val = jax.nn.sigmoid(values)
    return sigma_val * (1.0 + values * (1.0 - sigma_val))


def one_hot(index, count):
    return (index[..., None] == jnp.arange(count, dtype=index.dtype)).astype(BF16)


def split_dot(spec, left, right):
    return jnp.einsum(
        spec, left, right.astype(F32), precision=lax.Precision.HIGHEST, preferred_element_type=F32
    )


def all_sum(rows, owners):
    count, width = rows.shape
    unit = owners * 16
    length = -(-count // unit) * unit
    rows = jnp.pad(rows, ((0, length - count), (0, 0)))
    axes = ("group", "dom")
    mine = lax.all_to_all(
        rows.astype(BF16).reshape(owners, -1, width), axes, split_axis=0, concat_axis=0, tiled=True
    )
    mine = jnp.einsum(
        "o,orw->rw", jnp.ones((owners,), BF16), mine, preferred_element_type=F32
    ).astype(BF16)
    spread = jnp.broadcast_to(mine[None], (owners,) + mine.shape)
    gathered = lax.all_to_all(spread, axes, split_axis=0, concat_axis=0, tiled=True)
    return gathered.reshape(length, width)[:count].astype(F32)


def on_device(
    pin_feats,
    w_self,
    w_edge,
    w_head,
    w_out,
    send_rows,
    edge_src,
    edge_dst,
    pin_owner,
    pin_net,
    net_target,
):
    pin_count, feat_width = pin_feats.shape
    send_list = send_rows[0]
    halo_span = send_list.shape[0] // 2
    send_hot = one_hot(send_list, pin_count)
    outgoing = jnp.dot(send_hot, pin_feats, preferred_element_type=F32).astype(BF16)
    padded = extended(outgoing, (("dom", 0),), halo_span)
    node_table = jnp.concatenate([pin_feats, padded[:halo_span], padded[3 * halo_span :]], 0)
    table_rows = node_table.shape[0]
    sources = edge_src[0]
    endpoints = edge_dst[0]
    src_hot = one_hot(sources, table_rows)
    dst_hot = one_hot(endpoints, pin_count)
    gathered = jnp.einsum(
        "ter,rd->ted", src_hot, node_table, preferred_element_type=F32
    ).astype(BF16)
    edge_in = jnp.einsum("tep,ted->tpd", dst_hot, gathered, preferred_element_type=F32)
    summed = split_dot("tpk,tkd->pd", edge_in, w_edge)
    degree = jnp.sum(dst_hot.astype(F32), axis=(0, 1))
    inverse = 1.0 / (1.0 + degree)
    preact = (
        jnp.dot(pin_feats, w_self, preferred_element_type=F32) + summed * inverse[:, None]
    )
    hidden = jax.nn.silu(preact).astype(BF16)
    groups = lax.axis_size("group")
    domains = lax.axis_size("dom")
    owners = groups * domains
    capacity = max(2, 2 * pin_count // owners)
    net_count = net_target.shape[0]
    owner_ids = pin_owner[:, 0]
    owner_hot = one_hot(owner_ids, owners)
    earlier = (
        jnp.arange(pin_count, dtype=jnp.int32)[None, :]
        < jnp.arange(pin_count, dtype=jnp.int32)[:, None]
    ).astype(BF16)
    before = jnp.dot(earlier, owner_hot, preferred_element_type=F32)
    slot_rank = jnp.sum(before * owner_hot.astype(F32), axis=1).astype(jnp.int32)
    pin_slot = owner_ids * capacity + slot_rank
    slot_hot = one_hot(pin_slot, owners * capacity)
    net_code = (pin_net + 1).astype(BF16)[:, None]
    slot_nets = jnp.dot(slot_hot.T, net_code, preferred_element_type=F32)[:, 0] - 1.0
    outbound = jnp.dot(slot_hot.T, hidden, preferred_element_type=F32).astype(BF16)
    slot_nets_in = lax.all_to_all(
        slot_nets.astype(jnp.int32).reshape(owners, capacity),
        ("group", "dom"),
        split_axis=0,
        concat_axis=0,
        tiled=True,
    ).reshape(-1)
    inbound = lax.all_to_all(
        outbound.reshape(owners, capacity, feat_width),
        ("group", "dom"),
        split_axis=0,
        concat_axis=0,
        tiled=True,
    ).reshape(-1, feat_width)
    net_hot = one_hot(slot_nets_in, net_count)
    pooled = jnp.einsum("sn,sd->nd", net_hot, inbound, preferred_element_type=F32)
    pooled_b = pooled.astype(BF16)
    head_pre = jnp.dot(pooled_b, w_head, preferred_element_type=F32)
    activated = jax.nn.silu(head_pre).astype(BF16)
    predicted = jnp.dot(activated, w_out, preferred_element_type=F32)
    misfit = predicted - net_target
    head_grad = (
        misfit[:, None] * w_out.astype(F32)[None, :] * silu_slope(head_pre)
    ).astype(BF16)
    head_sum_t = jnp.einsum("nh,nd->hd", head_grad, pooled_b, preferred_element_type=F32)
    out_sum = jnp.dot(misfit, activated.astype(F32), precision=lax.Precision.HIGHEST)
    net_grad = jnp.einsum(
        "nh,dh->nd", head_grad, w_head, preferred_element_type=F32
    ).astype(BF16)
    returned = jnp.dot(net_hot, net_grad, preferred_element_type=F32).astype(BF16)
    arrived = lax.all_to_all(
        returned.reshape(owners, capacity, feat_width),
        ("group", "dom"),
        split_axis=0,
        concat_axis=0,
        tiled=True,
    ).reshape(-1, feat_width)
    pin_grad = jnp.dot(slot_hot, arrived, preferred_element_type=F32)
    preact_grad = (pin_grad * silu_slope(preact)).astype(BF16)
    self_sum = jnp.einsum("pk,pd->kd", pin_feats, preact_grad, preferred_element_type=F32)
    agg_grad = (preact_grad.astype(F32) * inverse[:, None]).astype(BF16)
    edge_rows = jnp.einsum(
        "tep,pd->ted", dst_hot, agg_grad, preferred_element_type=F32
    ).astype(BF16)
    edge_sum = jnp.einsum("tek,ted->tkd", gathered, edge_rows, preferred_element_type=F32)
    row_in = jnp.einsum("ter,ted->trd", src_hot, edge_rows, preferred_element_type=F32)
    table_grad = split_dot("trd,tkd->rk", row_in, w_edge)
    local_grad = (
        jnp.einsum("pd,kd->pk", preact_grad, w_self, preferred_element_type=F32)
        + table_grad[:pin_count]
    )
    halo_grad = table_grad[pin_count:].astype(BF16)
    back_padded = extended(halo_grad, (("dom", 0),), halo_span)
    received = jnp.concatenate([back_padded[:halo_span], back_padded[3 * halo_span :]], 0)
    grad_feats = (
        local_grad + jnp.einsum("sp,sd->pd", send_hot, received, preferred_element_type=F32)
    ).astype(BF16)
    head_width = head_sum_t.shape[0]
    pieces = (
        self_sum,
        edge_sum.reshape(-1, feat_width),
        head_sum_t,
        out_sum.reshape(-1, feat_width),
    )
    totals = all_sum(jnp.concatenate(pieces, 0), owners)
    grad_scale = 1.0 / math.sqrt(pin_count * owners)
    outs = []
    offset = 0
    for piece in pieces:
        outs.append(totals[offset : offset + piece.shape[0]] * grad_scale)
        offset += piece.shape[0]
    return (
        predicted,
        grad_feats,
        outs[0],
        outs[1].reshape(edge_sum.shape),
        outs[2].T,
        outs[3].reshape(head_width),
    )


def solution(mesh):
    in_specs = (
        P(("group", "dom"), None),
        P(),
        P(),
        P(),
        P(),
        P(("group", "dom"), None),
        P(("group", "dom"), None, None),
        P(("group", "dom"), None, None),
        P(("group", "dom"), None),
        P(("group", "dom")),
        P(("group", "dom")),
    )
    out_specs = (P(("group", "dom")), P(("group", "dom"), None), P(), P(), P(), P())
    return jax.shard_map(
        on_device, mesh=mesh, in_specs=in_specs, out_specs=out_specs, check_vma=False
    )
```

```python
import math

import jax
import jax.numpy as jnp
from jax import lax
from jax.sharding import PartitionSpec as P


F32 = jnp.float32
BF16 = jnp.bfloat16


def extended(block, sides, width):
    for axis, dim in sides:
        count = lax.axis_size(axis)
        forward = [(i, i + 1) for i in range(count - 1)]
        backward = [(target, source) for source, target in forward]
        low = lax.ppermute(
            lax.slice_in_dim(block, block.shape[dim] - width, None, axis=dim), axis, forward
        )
        high = lax.ppermute(lax.slice_in_dim(block, 0, width, axis=dim), axis, backward)
        block = jnp.concatenate([low, block, high], axis=dim)
    return block


def silu_slope(values):
    sigma_val = jax.nn.sigmoid(values)
    return sigma_val * (1.0 + values * (1.0 - sigma_val))


def one_hot(index, count):
    return (index[..., None] == jnp.arange(count, dtype=index.dtype)).astype(BF16)


def split_dot(spec, left, right):
    return jnp.einsum(
        spec, left, right.astype(F32), precision=lax.Precision.HIGHEST, preferred_element_type=F32
    )


def all_sum(rows, owners):
    count, width = rows.shape
    unit = owners * 16
    length = -(-count // unit) * unit
    rows = jnp.pad(rows, ((0, length - count), (0, 0)))
    axes = ("group", "dom")
    mine = lax.all_to_all(
        rows.astype(BF16).reshape(owners, -1, width), axes, split_axis=0, concat_axis=0, tiled=True
    )
    mine = jnp.einsum(
        "o,orw->rw", jnp.ones((owners,), BF16), mine, preferred_element_type=F32
    ).astype(BF16)
    spread = jnp.broadcast_to(mine[None], (owners,) + mine.shape)
    gathered = lax.all_to_all(spread, axes, split_axis=0, concat_axis=0, tiled=True)
    return gathered.reshape(length, width)[:count].astype(F32)


def on_device(
    pin_feats,
    w_self,
    w_edge,
    w_head,
    w_out,
    send_rows,
    edge_src,
    edge_dst,
    pin_owner,
    pin_net,
    net_target,
):
    pin_count, feat_width = pin_feats.shape
    send_list = send_rows[0]
    halo_span = send_list.shape[0] // 2
    send_hot = one_hot(send_list, pin_count)
    outgoing = jnp.dot(send_hot, pin_feats, preferred_element_type=F32).astype(BF16)
    padded = extended(outgoing, (("dom", 0),), halo_span)
    node_table = jnp.concatenate([pin_feats, padded[:halo_span], padded[3 * halo_span :]], 0)
    table_rows = node_table.shape[0]
    sources = edge_src[0]
    endpoints = edge_dst[0]
    src_hot = one_hot(sources, table_rows)
    dst_hot = one_hot(endpoints, pin_count)
    gathered = jnp.einsum(
        "ter,rd->ted", src_hot, node_table, preferred_element_type=F32
    ).astype(BF16)
    edge_in = jnp.einsum("tep,ted->tpd", dst_hot, gathered, preferred_element_type=F32)
    summed = split_dot("tpk,tkd->pd", edge_in, w_edge)
    degree = jnp.sum(dst_hot.astype(F32), axis=(0, 1))
    inverse = 1.0 / (1.0 + degree)
    preact = (
        jnp.dot(pin_feats, w_self, preferred_element_type=F32) + summed * inverse[:, None]
    )
    hidden = jax.nn.silu(preact).astype(BF16)
    groups = lax.axis_size("group")
    domains = lax.axis_size("dom")
    owners = groups * domains
    capacity = max(2, 2 * pin_count // owners)
    net_count = net_target.shape[0]
    owner_ids = pin_owner[:, 0]
    owner_hot = one_hot(owner_ids, owners)
    earlier = (
        jnp.arange(pin_count, dtype=jnp.int32)[None, :]
        < jnp.arange(pin_count, dtype=jnp.int32)[:, None]
    ).astype(BF16)
    before = jnp.dot(earlier, owner_hot, preferred_element_type=F32)
    slot_rank = jnp.sum(before * owner_hot.astype(F32), axis=1).astype(jnp.int32)
    pin_slot = owner_ids * capacity + slot_rank
    slot_hot = one_hot(pin_slot, owners * capacity)
    net_code = (pin_net + 1).astype(BF16)[:, None]
    slot_nets = jnp.dot(slot_hot.T, net_code, preferred_element_type=F32)[:, 0] - 1.0
    outbound = jnp.dot(slot_hot.T, hidden, preferred_element_type=F32).astype(BF16)
    id_rows = -(-capacity // (8 * feat_width)) * 8
    id_block = jnp.pad(
        slot_nets.reshape(owners, capacity), ((0, 0), (0, id_rows * feat_width - capacity))
    ).astype(BF16)
    packet = jnp.concatenate(
        [
            outbound.reshape(owners, capacity, feat_width),
            id_block.reshape(owners, id_rows, feat_width),
        ],
        1,
    )
    packet_in = lax.all_to_all(packet, ("group", "dom"), split_axis=0, concat_axis=0, tiled=True)
    inbound = packet_in[:, :capacity].reshape(-1, feat_width)
    slot_nets_in = (
        packet_in[:, capacity:].reshape(owners, -1)[:, :capacity].astype(F32).astype(jnp.int32)
    ).reshape(-1)
    net_hot = one_hot(slot_nets_in, net_count)
    pooled = jnp.einsum("sn,sd->nd", net_hot, inbound, preferred_element_type=F32)
    pooled_b = pooled.astype(BF16)
    head_pre = jnp.dot(pooled_b, w_head, preferred_element_type=F32)
    activated = jax.nn.silu(head_pre).astype(BF16)
    predicted = jnp.dot(activated, w_out, preferred_element_type=F32)
    misfit = predicted - net_target
    head_grad = (
        misfit[:, None] * w_out.astype(F32)[None, :] * silu_slope(head_pre)
    ).astype(BF16)
    head_sum_t = jnp.einsum("nh,nd->hd", head_grad, pooled_b, preferred_element_type=F32)
    out_sum = jnp.dot(misfit, activated.astype(F32), precision=lax.Precision.HIGHEST)
    net_grad = jnp.einsum(
        "nh,dh->nd", head_grad, w_head, preferred_element_type=F32
    ).astype(BF16)
    returned = jnp.dot(net_hot, net_grad, preferred_element_type=F32).astype(BF16)
    arrived = lax.all_to_all(
        returned.reshape(owners, capacity, feat_width),
        ("group", "dom"),
        split_axis=0,
        concat_axis=0,
        tiled=True,
    ).reshape(-1, feat_width)
    pin_grad = jnp.dot(slot_hot, arrived, preferred_element_type=F32)
    preact_grad = (pin_grad * silu_slope(preact)).astype(BF16)
    self_sum = jnp.einsum("pk,pd->kd", pin_feats, preact_grad, preferred_element_type=F32)
    agg_grad = (preact_grad.astype(F32) * inverse[:, None]).astype(BF16)
    edge_rows = jnp.einsum(
        "tep,pd->ted", dst_hot, agg_grad, preferred_element_type=F32
    ).astype(BF16)
    edge_sum = jnp.einsum("tek,ted->tkd", gathered, edge_rows, preferred_element_type=F32)
    row_in = jnp.einsum("ter,ted->trd", src_hot, edge_rows, preferred_element_type=F32)
    table_grad = split_dot("trd,tkd->rk", row_in, w_edge)
    local_grad = (
        jnp.einsum("pd,kd->pk", preact_grad, w_self, preferred_element_type=F32)
        + table_grad[:pin_count]
    )
    halo_grad = table_grad[pin_count:].astype(BF16)
    back_padded = extended(halo_grad, (("dom", 0),), halo_span)
    received = jnp.concatenate([back_padded[:halo_span], back_padded[3 * halo_span :]], 0)
    grad_feats = (
        local_grad + jnp.einsum("sp,sd->pd", send_hot, received, preferred_element_type=F32)
    ).astype(BF16)
    head_width = head_sum_t.shape[0]
    pieces = (
        self_sum,
        edge_sum.reshape(-1, feat_width),
        head_sum_t,
        out_sum.reshape(-1, feat_width),
    )
    totals = all_sum(jnp.concatenate(pieces, 0), owners)
    grad_scale = 1.0 / math.sqrt(pin_count * owners)
    outs = []
    offset = 0
    for piece in pieces:
        outs.append(totals[offset : offset + piece.shape[0]] * grad_scale)
        offset += piece.shape[0]
    return (
        predicted,
        grad_feats,
        outs[0],
        outs[1].reshape(edge_sum.shape),
        outs[2].T,
        outs[3].reshape(head_width),
    )


def solution(mesh):
    in_specs = (
        P(("group", "dom"), None),
        P(),
        P(),
        P(),
        P(),
        P(("group", "dom"), None),
        P(("group", "dom"), None, None),
        P(("group", "dom"), None, None),
        P(("group", "dom"), None),
        P(("group", "dom")),
        P(("group", "dom")),
    )
    out_specs = (P(("group", "dom")), P(("group", "dom"), None), P(), P(), P(), P())
    return jax.shard_map(
        on_device, mesh=mesh, in_specs=in_specs, out_specs=out_specs, check_vma=False
    )
```

```python
import math

import jax
import jax.numpy as jnp
from jax import lax
from jax.sharding import PartitionSpec as P


F32 = jnp.float32
BF16 = jnp.bfloat16


def extended(block, sides, width):
    for axis, dim in sides:
        count = lax.axis_size(axis)
        forward = [(i, i + 1) for i in range(count - 1)]
        backward = [(target, source) for source, target in forward]
        low = lax.ppermute(
            lax.slice_in_dim(block, block.shape[dim] - width, None, axis=dim), axis, forward
        )
        high = lax.ppermute(lax.slice_in_dim(block, 0, width, axis=dim), axis, backward)
        block = jnp.concatenate([low, block, high], axis=dim)
    return block


def silu_slope(values):
    sigma_val = jax.nn.sigmoid(values)
    return sigma_val * (1.0 + values * (1.0 - sigma_val))


def one_hot(index, count):
    return (index[..., None] == jnp.arange(count, dtype=index.dtype)).astype(BF16)


def split_dot(spec, left, right):
    return jnp.einsum(
        spec, left, right.astype(F32), precision=lax.Precision.HIGHEST, preferred_element_type=F32
    )


def all_sum(rows, owners):
    count, width = rows.shape
    unit = owners * 8
    length = -(-count // unit) * unit
    rows = jnp.pad(rows, ((0, length - count), (0, 0)))
    axes = ("group", "dom")
    mine = lax.all_to_all(
        rows.astype(BF16).reshape(owners, -1, width), axes, split_axis=0, concat_axis=0, tiled=True
    )
    mine = jnp.einsum(
        "o,orw->rw", jnp.ones((owners,), BF16), mine, preferred_element_type=F32
    ).astype(BF16)
    spread = jnp.broadcast_to(mine[None], (owners,) + mine.shape)
    gathered = lax.all_to_all(spread, axes, split_axis=0, concat_axis=0, tiled=True)
    return gathered.reshape(length, width)[:count].astype(F32)


def on_device(
    pin_feats,
    w_self,
    w_edge,
    w_head,
    w_out,
    send_rows,
    edge_src,
    edge_dst,
    pin_owner,
    pin_net,
    net_target,
):
    pin_count, feat_width = pin_feats.shape
    send_list = send_rows[0]
    halo_span = send_list.shape[0] // 2
    send_hot = one_hot(send_list, pin_count)
    outgoing = jnp.dot(send_hot, pin_feats, preferred_element_type=F32).astype(BF16)
    padded = extended(outgoing, (("dom", 0),), halo_span)
    node_table = jnp.concatenate([pin_feats, padded[:halo_span], padded[3 * halo_span :]], 0)
    table_rows = node_table.shape[0]
    sources = edge_src[0]
    endpoints = edge_dst[0]
    src_hot = one_hot(sources, table_rows)
    dst_hot = one_hot(endpoints, pin_count)
    gathered = jnp.einsum(
        "ter,rd->ted", src_hot, node_table, preferred_element_type=F32
    ).astype(BF16)
    edge_in = jnp.einsum("tep,ted->tpd", dst_hot, gathered, preferred_element_type=F32)
    summed = split_dot("tpk,tkd->pd", edge_in, w_edge)
    degree = jnp.sum(dst_hot.astype(F32), axis=(0, 1))
    inverse = 1.0 / (1.0 + degree)
    preact = (
        jnp.dot(pin_feats, w_self, preferred_element_type=F32) + summed * inverse[:, None]
    )
    hidden = jax.nn.silu(preact).astype(BF16)
    groups = lax.axis_size("group")
    domains = lax.axis_size("dom")
    owners = groups * domains
    capacity = max(2, 2 * pin_count // owners)
    net_count = net_target.shape[0]
    owner_ids = pin_owner[:, 0]
    owner_hot = one_hot(owner_ids, owners)
    earlier = (
        jnp.arange(pin_count, dtype=jnp.int32)[None, :]
        < jnp.arange(pin_count, dtype=jnp.int32)[:, None]
    ).astype(BF16)
    before = jnp.dot(earlier, owner_hot, preferred_element_type=F32)
    slot_rank = jnp.sum(before * owner_hot.astype(F32), axis=1).astype(jnp.int32)
    pin_slot = owner_ids * capacity + slot_rank
    slot_hot = one_hot(pin_slot, owners * capacity)
    net_code = (pin_net + 1).astype(BF16)[:, None]
    slot_nets = jnp.dot(slot_hot.T, net_code, preferred_element_type=F32)[:, 0] - 1.0
    outbound = jnp.dot(slot_hot.T, hidden, preferred_element_type=F32).astype(BF16)
    id_rows = -(-capacity // (8 * feat_width)) * 8
    id_block = jnp.pad(
        slot_nets.reshape(owners, capacity), ((0, 0), (0, id_rows * feat_width - capacity))
    ).astype(BF16)
    packet = jnp.concatenate(
        [
            outbound.reshape(owners, capacity, feat_width),
            id_block.reshape(owners, id_rows, feat_width),
        ],
        1,
    )
    packet_in = lax.all_to_all(packet, ("group", "dom"), split_axis=0, concat_axis=0, tiled=True)
    inbound = packet_in[:, :capacity].reshape(-1, feat_width)
    slot_nets_in = (
        packet_in[:, capacity:].reshape(owners, -1)[:, :capacity].astype(F32).astype(jnp.int32)
    ).reshape(-1)
    net_hot = one_hot(slot_nets_in, net_count)
    pooled = jnp.einsum("sn,sd->nd", net_hot, inbound, preferred_element_type=F32)
    pooled_b = pooled.astype(BF16)
    head_pre = jnp.dot(pooled_b, w_head, preferred_element_type=F32)
    activated = jax.nn.silu(head_pre).astype(BF16)
    predicted = jnp.dot(activated, w_out, preferred_element_type=F32)
    misfit = predicted - net_target
    head_grad = (
        misfit[:, None] * w_out.astype(F32)[None, :] * silu_slope(head_pre)
    ).astype(BF16)
    head_sum_t = jnp.einsum("nh,nd->hd", head_grad, pooled_b, preferred_element_type=F32)
    out_sum = jnp.dot(misfit, activated.astype(F32), precision=lax.Precision.HIGHEST)
    net_grad = jnp.einsum(
        "nh,dh->nd", head_grad, w_head, preferred_element_type=F32
    ).astype(BF16)
    returned = jnp.dot(net_hot, net_grad, preferred_element_type=F32).astype(BF16)
    out_rows = out_sum.reshape(-1, feat_width).astype(BF16)
    back_rows = -(-(capacity + out_rows.shape[0]) // 8) * 8
    back_packet = jnp.concatenate(
        [
            returned.reshape(owners, capacity, feat_width),
            jnp.broadcast_to(out_rows[None], (owners,) + out_rows.shape),
            jnp.zeros(
                (owners, back_rows - capacity - out_rows.shape[0], feat_width), BF16
            ),
        ],
        1,
    )
    back_in = lax.all_to_all(
        back_packet, ("group", "dom"), split_axis=0, concat_axis=0, tiled=True
    )
    arrived = back_in[:, :capacity].reshape(-1, feat_width)
    out_total = jnp.einsum(
        "o,orw->rw",
        jnp.ones((owners,), BF16),
        back_in[:, capacity : capacity + out_rows.shape[0]],
        preferred_element_type=F32,
    ).reshape(-1)
    pin_grad = jnp.dot(slot_hot, arrived, preferred_element_type=F32)
    preact_grad = (pin_grad * silu_slope(preact)).astype(BF16)
    self_sum = jnp.einsum("pk,pd->kd", pin_feats, preact_grad, preferred_element_type=F32)
    agg_grad = (preact_grad.astype(F32) * inverse[:, None]).astype(BF16)
    edge_rows = jnp.einsum(
        "tep,pd->ted", dst_hot, agg_grad, preferred_element_type=F32
    ).astype(BF16)
    edge_sum = jnp.einsum("tek,ted->tkd", gathered, edge_rows, preferred_element_type=F32)
    row_in = jnp.einsum("ter,ted->trd", src_hot, edge_rows, preferred_element_type=F32)
    table_grad = split_dot("trd,tkd->rk", row_in, w_edge)
    local_grad = (
        jnp.einsum("pd,kd->pk", preact_grad, w_self, preferred_element_type=F32)
        + table_grad[:pin_count]
    )
    halo_grad = table_grad[pin_count:].astype(BF16)
    back_padded = extended(halo_grad, (("dom", 0),), halo_span)
    received = jnp.concatenate([back_padded[:halo_span], back_padded[3 * halo_span :]], 0)
    grad_feats = (
        local_grad + jnp.einsum("sp,sd->pd", send_hot, received, preferred_element_type=F32)
    ).astype(BF16)
    pieces = (self_sum, edge_sum.reshape(-1, feat_width), head_sum_t)
    totals = all_sum(jnp.concatenate(pieces, 0), owners)
    grad_scale = 1.0 / math.sqrt(pin_count * owners)
    outs = []
    offset = 0
    for piece in pieces:
        outs.append(totals[offset : offset + piece.shape[0]] * grad_scale)
        offset += piece.shape[0]
    return (
        predicted,
        grad_feats,
        outs[0],
        outs[1].reshape(edge_sum.shape),
        outs[2].T,
        out_total * grad_scale,
    )


def solution(mesh):
    in_specs = (
        P(("group", "dom"), None),
        P(),
        P(),
        P(),
        P(),
        P(("group", "dom"), None),
        P(("group", "dom"), None, None),
        P(("group", "dom"), None, None),
        P(("group", "dom"), None),
        P(("group", "dom")),
        P(("group", "dom")),
    )
    out_specs = (P(("group", "dom")), P(("group", "dom"), None), P(), P(), P(), P())
    return jax.shard_map(
        on_device, mesh=mesh, in_specs=in_specs, out_specs=out_specs, check_vma=False
    )
```

```python
import math

import jax
import jax.numpy as jnp
from jax import lax
from jax.sharding import PartitionSpec as P


F32 = jnp.float32
BF16 = jnp.bfloat16


DOM = ("zdom", "core")
ALL = ("group",) + DOM
CHIP = ("group", "zdom")


def size_of(axes):
    return math.prod(lax.axis_size(axis) for axis in axes)


def extended(block, sides, width):
    for axis, dim in sides:
        count = size_of(axis)
        forward = [(i, i + 1) for i in range(count - 1)]
        backward = [(target, source) for source, target in forward]
        low = lax.ppermute(
            lax.slice_in_dim(block, block.shape[dim] - width, None, axis=dim), axis, forward
        )
        high = lax.ppermute(lax.slice_in_dim(block, 0, width, axis=dim), axis, backward)
        block = jnp.concatenate([low, block, high], axis=dim)
    return block


def silu_slope(values):
    sigma_val = jax.nn.sigmoid(values)
    return sigma_val * (1.0 + values * (1.0 - sigma_val))


def one_hot(index, count):
    return (index[..., None] == jnp.arange(count, dtype=index.dtype)).astype(BF16)


def split_dot(spec, left, right):
    return jnp.einsum(
        spec, left, right.astype(F32), precision=lax.Precision.HIGHEST, preferred_element_type=F32
    )


def all_sum(rows, owners):
    count, width = rows.shape
    chips = size_of(CHIP)
    cores = lax.axis_size("core")
    unit = chips * cores * 8
    length = -(-count // unit) * unit
    rows = jnp.pad(rows, ((0, length - count), (0, 0))).reshape(cores, length // cores, width)
    core = lax.axis_index("core")
    swap = [(i, (i + 1) % cores) for i in range(cores)]
    kept = lax.dynamic_index_in_dim(rows, core, 0, keepdims=False)
    given = lax.dynamic_index_in_dim(rows, (core + 1) % cores, 0, keepdims=False)
    half = kept + lax.ppermute(given, "core", swap)
    mine = lax.all_to_all(
        half.astype(BF16).reshape(chips, -1, width), CHIP, split_axis=0, concat_axis=0, tiled=True
    )
    mine = jnp.einsum(
        "o,orw->rw", jnp.ones((chips,), BF16), mine, preferred_element_type=F32
    ).astype(BF16)
    spread = jnp.broadcast_to(mine[None], (chips,) + mine.shape)
    own_half = lax.all_to_all(spread, CHIP, split_axis=0, concat_axis=0, tiled=True).reshape(
        -1, width
    )
    other_half = lax.ppermute(own_half, "core", swap)
    first = jnp.where(core == 0, own_half, other_half)
    second = jnp.where(core == 0, other_half, own_half)
    return jnp.concatenate([first, second], 0)[:count].astype(F32)


def on_device(
    pin_feats,
    w_self,
    w_edge,
    w_head,
    w_out,
    send_rows,
    edge_src,
    edge_dst,
    pin_owner,
    pin_net,
    net_target,
):
    pin_count, feat_width = pin_feats.shape
    send_list = send_rows[0]
    halo_span = send_list.shape[0] // 2
    send_hot = one_hot(send_list, pin_count)
    outgoing = jnp.dot(send_hot, pin_feats, preferred_element_type=F32).astype(BF16)
    padded = extended(outgoing, ((DOM, 0),), halo_span)
    node_table = jnp.concatenate([pin_feats, padded[:halo_span], padded[3 * halo_span :]], 0)
    table_rows = node_table.shape[0]
    sources = edge_src[0]
    endpoints = edge_dst[0]
    src_hot = one_hot(sources, table_rows)
    dst_hot = one_hot(endpoints, pin_count)
    gathered = jnp.einsum(
        "ter,rd->ted", src_hot, node_table, preferred_element_type=F32
    ).astype(BF16)
    edge_in = jnp.einsum("tep,ted->tpd", dst_hot, gathered, preferred_element_type=F32)
    summed = split_dot("tpk,tkd->pd", edge_in, w_edge)
    degree = jnp.sum(dst_hot.astype(F32), axis=(0, 1))
    inverse = 1.0 / (1.0 + degree)
    preact = (
        jnp.dot(pin_feats, w_self, preferred_element_type=F32) + summed * inverse[:, None]
    )
    hidden = jax.nn.silu(preact).astype(BF16)
    groups = lax.axis_size("group")
    domains = size_of(DOM)
    owners = groups * domains
    capacity = max(2, 2 * pin_count // owners)
    net_count = net_target.shape[0]
    owner_ids = pin_owner[:, 0]
    owner_hot = one_hot(owner_ids, owners)
    earlier = (
        jnp.arange(pin_count, dtype=jnp.int32)[None, :]
        < jnp.arange(pin_count, dtype=jnp.int32)[:, None]
    ).astype(BF16)
    before = jnp.dot(earlier, owner_hot, preferred_element_type=F32)
    slot_rank = jnp.sum(before * owner_hot.astype(F32), axis=1).astype(jnp.int32)
    pin_slot = owner_ids * capacity + slot_rank
    slot_hot = one_hot(pin_slot, owners * capacity)
    net_code = (pin_net + 1).astype(BF16)[:, None]
    slot_nets = jnp.dot(slot_hot.T, net_code, preferred_element_type=F32)[:, 0] - 1.0
    outbound = jnp.dot(slot_hot.T, hidden, preferred_element_type=F32).astype(BF16)
    id_rows = -(-capacity // (8 * feat_width)) * 8
    id_block = jnp.pad(
        slot_nets.reshape(owners, capacity), ((0, 0), (0, id_rows * feat_width - capacity))
    ).astype(BF16)
    packet = jnp.concatenate(
        [
            outbound.reshape(owners, capacity, feat_width),
            id_block.reshape(owners, id_rows, feat_width),
        ],
        1,
    )
    packet_in = lax.all_to_all(packet, ALL, split_axis=0, concat_axis=0, tiled=True)
    inbound = packet_in[:, :capacity].reshape(-1, feat_width)
    slot_nets_in = (
        packet_in[:, capacity:].reshape(owners, -1)[:, :capacity].astype(F32).astype(jnp.int32)
    ).reshape(-1)
    net_hot = one_hot(slot_nets_in, net_count)
    pooled = jnp.einsum("sn,sd->nd", net_hot, inbound, preferred_element_type=F32)
    pooled_b = pooled.astype(BF16)
    head_pre = jnp.dot(pooled_b, w_head, preferred_element_type=F32)
    activated = jax.nn.silu(head_pre).astype(BF16)
    predicted = jnp.dot(activated, w_out, preferred_element_type=F32)
    misfit = predicted - net_target
    head_grad = (
        misfit[:, None] * w_out.astype(F32)[None, :] * silu_slope(head_pre)
    ).astype(BF16)
    head_sum_t = jnp.einsum("nh,nd->hd", head_grad, pooled_b, preferred_element_type=F32)
    out_sum = jnp.dot(misfit, activated.astype(F32), precision=lax.Precision.HIGHEST)
    net_grad = jnp.einsum(
        "nh,dh->nd", head_grad, w_head, preferred_element_type=F32
    ).astype(BF16)
    returned = jnp.dot(net_hot, net_grad, preferred_element_type=F32).astype(BF16)
    out_rows = out_sum.reshape(-1, feat_width).astype(BF16)
    back_rows = -(-(capacity + out_rows.shape[0]) // 8) * 8
    back_packet = jnp.concatenate(
        [
            returned.reshape(owners, capacity, feat_width),
            jnp.broadcast_to(out_rows[None], (owners,) + out_rows.shape),
            jnp.zeros(
                (owners, back_rows - capacity - out_rows.shape[0], feat_width), BF16
            ),
        ],
        1,
    )
    back_in = lax.all_to_all(
        back_packet, ALL, split_axis=0, concat_axis=0, tiled=True
    )
    arrived = back_in[:, :capacity].reshape(-1, feat_width)
    out_total = jnp.einsum(
        "o,orw->rw",
        jnp.ones((owners,), BF16),
        back_in[:, capacity : capacity + out_rows.shape[0]],
        preferred_element_type=F32,
    ).reshape(-1)
    pin_grad = jnp.dot(slot_hot, arrived, preferred_element_type=F32)
    preact_grad = (pin_grad * silu_slope(preact)).astype(BF16)
    self_sum = jnp.einsum("pk,pd->kd", pin_feats, preact_grad, preferred_element_type=F32)
    agg_grad = (preact_grad.astype(F32) * inverse[:, None]).astype(BF16)
    edge_rows = jnp.einsum(
        "tep,pd->ted", dst_hot, agg_grad, preferred_element_type=F32
    ).astype(BF16)
    edge_sum = jnp.einsum("tek,ted->tkd", gathered, edge_rows, preferred_element_type=F32)
    row_in = jnp.einsum("ter,ted->trd", src_hot, edge_rows, preferred_element_type=F32)
    table_grad = split_dot("trd,tkd->rk", row_in, w_edge)
    local_grad = (
        jnp.einsum("pd,kd->pk", preact_grad, w_self, preferred_element_type=F32)
        + table_grad[:pin_count]
    )
    halo_grad = table_grad[pin_count:].astype(BF16)
    back_padded = extended(halo_grad, ((DOM, 0),), halo_span)
    received = jnp.concatenate([back_padded[:halo_span], back_padded[3 * halo_span :]], 0)
    grad_feats = (
        local_grad + jnp.einsum("sp,sd->pd", send_hot, received, preferred_element_type=F32)
    ).astype(BF16)
    pieces = (self_sum, edge_sum.reshape(-1, feat_width), head_sum_t)
    totals = all_sum(jnp.concatenate(pieces, 0), owners)
    grad_scale = 1.0 / math.sqrt(pin_count * owners)
    outs = []
    offset = 0
    for piece in pieces:
        outs.append(totals[offset : offset + piece.shape[0]] * grad_scale)
        offset += piece.shape[0]
    return (
        predicted,
        grad_feats,
        outs[0],
        outs[1].reshape(edge_sum.shape),
        outs[2].T,
        out_total * grad_scale,
    )


def solution(mesh):
    in_specs = (
        P(ALL, None),
        P(),
        P(),
        P(),
        P(),
        P(ALL, None),
        P(ALL, None, None),
        P(ALL, None, None),
        P(ALL, None),
        P(ALL),
        P(ALL),
    )
    out_specs = (P(ALL), P(ALL, None), P(), P(), P(), P())
    shape = mesh.devices.shape
    cores = 2
    chip_mesh = jax.sharding.Mesh(
        mesh.devices.reshape(shape[0], shape[1] // cores, cores), ("group", "zdom", "core")
    )
    return jax.shard_map(
        on_device, mesh=chip_mesh, in_specs=in_specs, out_specs=out_specs, check_vma=False
    )
```

```python
import math

import jax
import jax.numpy as jnp
from jax import lax
from jax.sharding import PartitionSpec as P


F32 = jnp.float32
BF16 = jnp.bfloat16


DOM = ("zdom", "core")
ALL = ("group",) + DOM
CHIP = ("group", "zdom")


def size_of(axes):
    return math.prod(lax.axis_size(axis) for axis in axes)


def extended(block, sides, width):
    for axis, dim in sides:
        count = size_of(axis)
        forward = [(i, i + 1) for i in range(count - 1)]
        backward = [(target, source) for source, target in forward]
        low = lax.ppermute(
            lax.slice_in_dim(block, block.shape[dim] - width, None, axis=dim), axis, forward
        )
        high = lax.ppermute(lax.slice_in_dim(block, 0, width, axis=dim), axis, backward)
        block = jnp.concatenate([low, block, high], axis=dim)
    return block


def silu_slope(values):
    sigma_val = jax.nn.sigmoid(values)
    return sigma_val * (1.0 + values * (1.0 - sigma_val))


def one_hot(index, count):
    return (index[..., None] == jnp.arange(count, dtype=index.dtype)).astype(BF16)


def one_hot_rows(index, count):
    return (jnp.arange(count, dtype=index.dtype)[:, None] == index[..., None, :]).astype(BF16)


def split_dot(spec, left, right):
    return jnp.einsum(
        spec, left, right.astype(F32), precision=lax.Precision.HIGHEST, preferred_element_type=F32
    )


def all_sum(rows, owners):
    count, width = rows.shape
    chips = size_of(CHIP)
    cores = lax.axis_size("core")
    unit = chips * cores * 8
    length = -(-count // unit) * unit
    rows = jnp.pad(rows, ((0, length - count), (0, 0))).reshape(cores, length // cores, width)
    core = lax.axis_index("core")
    swap = [(i, (i + 1) % cores) for i in range(cores)]
    kept = lax.dynamic_index_in_dim(rows, core, 0, keepdims=False)
    given = lax.dynamic_index_in_dim(rows, (core + 1) % cores, 0, keepdims=False)
    half = kept + lax.ppermute(given, "core", swap)
    mine = lax.all_to_all(
        half.astype(BF16).reshape(chips, -1, width), CHIP, split_axis=0, concat_axis=0, tiled=True
    )
    mine = jnp.einsum(
        "o,orw->rw", jnp.ones((chips,), BF16), mine, preferred_element_type=F32
    ).astype(BF16)
    spread = jnp.broadcast_to(mine[None], (chips,) + mine.shape)
    own_half = lax.all_to_all(spread, CHIP, split_axis=0, concat_axis=0, tiled=True).reshape(
        -1, width
    )
    other_half = lax.ppermute(own_half, "core", swap)
    first = jnp.where(core == 0, own_half, other_half)
    second = jnp.where(core == 0, other_half, own_half)
    return jnp.concatenate([first, second], 0)[:count].astype(F32)


def on_device(
    pin_feats,
    w_self,
    w_edge,
    w_head,
    w_out,
    send_rows,
    edge_src,
    edge_dst,
    pin_owner,
    pin_net,
    net_target,
):
    pin_count, feat_width = pin_feats.shape
    send_list = send_rows[0]
    halo_span = send_list.shape[0] // 2
    send_hot = one_hot(send_list, pin_count)
    outgoing = jnp.dot(send_hot, pin_feats, preferred_element_type=F32).astype(BF16)
    padded = extended(outgoing, ((DOM, 0),), halo_span)
    node_table = jnp.concatenate([pin_feats, padded[:halo_span], padded[3 * halo_span :]], 0)
    table_rows = node_table.shape[0]
    sources = edge_src[0]
    endpoints = edge_dst[0]
    src_hot = one_hot(sources, table_rows)
    dst_hot = one_hot(endpoints, pin_count)
    gathered = jnp.einsum(
        "ter,rd->ted", src_hot, node_table, preferred_element_type=F32
    ).astype(BF16)
    edge_in = jnp.einsum(
        "tpe,ted->tpd", one_hot_rows(endpoints, pin_count), gathered, preferred_element_type=F32
    )
    summed = split_dot("tpk,tkd->pd", edge_in, w_edge)
    degree = jnp.sum(dst_hot.astype(F32), axis=(0, 1))
    inverse = 1.0 / (1.0 + degree)
    preact = (
        jnp.dot(pin_feats, w_self, preferred_element_type=F32) + summed * inverse[:, None]
    )
    hidden = jax.nn.silu(preact).astype(BF16)
    groups = lax.axis_size("group")
    domains = size_of(DOM)
    owners = groups * domains
    capacity = max(2, 2 * pin_count // owners)
    net_count = net_target.shape[0]
    owner_ids = pin_owner[:, 0]
    owner_hot = one_hot(owner_ids, owners)
    earlier = (
        jnp.arange(pin_count, dtype=jnp.int32)[None, :]
        < jnp.arange(pin_count, dtype=jnp.int32)[:, None]
    ).astype(BF16)
    before = jnp.dot(earlier, owner_hot, preferred_element_type=F32)
    slot_rank = jnp.sum(before * owner_hot.astype(F32), axis=1).astype(jnp.int32)
    pin_slot = owner_ids * capacity + slot_rank
    slot_hot = one_hot(pin_slot, owners * capacity)
    net_code = (pin_net + 1).astype(BF16)[:, None]
    slot_rows = one_hot_rows(pin_slot, owners * capacity)
    slot_nets = jnp.dot(slot_rows, net_code, preferred_element_type=F32)[:, 0] - 1.0
    outbound = jnp.dot(slot_rows, hidden, preferred_element_type=F32).astype(BF16)
    id_rows = -(-capacity // (8 * feat_width)) * 8
    id_block = jnp.pad(
        slot_nets.reshape(owners, capacity), ((0, 0), (0, id_rows * feat_width - capacity))
    ).astype(BF16)
    packet = jnp.concatenate(
        [
            outbound.reshape(owners, capacity, feat_width),
            id_block.reshape(owners, id_rows, feat_width),
        ],
        1,
    )
    packet_in = lax.all_to_all(packet, ALL, split_axis=0, concat_axis=0, tiled=True)
    inbound = packet_in[:, :capacity].reshape(-1, feat_width)
    slot_nets_in = (
        packet_in[:, capacity:].reshape(owners, -1)[:, :capacity].astype(F32).astype(jnp.int32)
    ).reshape(-1)
    net_hot = one_hot(slot_nets_in, net_count)
    pooled = jnp.dot(
        one_hot_rows(slot_nets_in, net_count), inbound, preferred_element_type=F32
    )
    pooled_b = pooled.astype(BF16)
    head_pre = jnp.dot(pooled_b, w_head, preferred_element_type=F32)
    activated = jax.nn.silu(head_pre).astype(BF16)
    predicted = jnp.dot(activated, w_out, preferred_element_type=F32)
    misfit = predicted - net_target
    head_grad = (
        misfit[:, None] * w_out.astype(F32)[None, :] * silu_slope(head_pre)
    ).astype(BF16)
    head_sum_t = jnp.einsum("nh,nd->hd", head_grad, pooled_b, preferred_element_type=F32)
    out_sum = jnp.dot(misfit, activated.astype(F32), precision=lax.Precision.HIGHEST)
    net_grad = jnp.einsum(
        "nh,dh->nd", head_grad, w_head, preferred_element_type=F32
    ).astype(BF16)
    returned = jnp.dot(net_hot, net_grad, preferred_element_type=F32).astype(BF16)
    out_rows = out_sum.reshape(-1, feat_width).astype(BF16)
    back_rows = -(-(capacity + out_rows.shape[0]) // 8) * 8
    back_packet = jnp.concatenate(
        [
            returned.reshape(owners, capacity, feat_width),
            jnp.broadcast_to(out_rows[None], (owners,) + out_rows.shape),
            jnp.zeros(
                (owners, back_rows - capacity - out_rows.shape[0], feat_width), BF16
            ),
        ],
        1,
    )
    back_in = lax.all_to_all(
        back_packet, ALL, split_axis=0, concat_axis=0, tiled=True
    )
    arrived = back_in[:, :capacity].reshape(-1, feat_width)
    out_total = jnp.einsum(
        "o,orw->rw",
        jnp.ones((owners,), BF16),
        back_in[:, capacity : capacity + out_rows.shape[0]],
        preferred_element_type=F32,
    ).reshape(-1)
    pin_grad = jnp.dot(slot_hot, arrived, preferred_element_type=F32)
    preact_grad = (pin_grad * silu_slope(preact)).astype(BF16)
    self_sum = jnp.einsum("pk,pd->kd", pin_feats, preact_grad, preferred_element_type=F32)
    agg_grad = (preact_grad.astype(F32) * inverse[:, None]).astype(BF16)
    edge_rows = jnp.einsum(
        "tep,pd->ted", dst_hot, agg_grad, preferred_element_type=F32
    ).astype(BF16)
    edge_sum = jnp.einsum("tek,ted->tkd", gathered, edge_rows, preferred_element_type=F32)
    row_in = jnp.einsum(
        "tre,ted->trd", one_hot_rows(sources, table_rows), edge_rows, preferred_element_type=F32
    )
    table_grad = split_dot("trd,tkd->rk", row_in, w_edge)
    local_grad = (
        jnp.einsum("pd,kd->pk", preact_grad, w_self, preferred_element_type=F32)
        + table_grad[:pin_count]
    )
    halo_grad = table_grad[pin_count:].astype(BF16)
    back_padded = extended(halo_grad, ((DOM, 0),), halo_span)
    received = jnp.concatenate([back_padded[:halo_span], back_padded[3 * halo_span :]], 0)
    grad_feats = (
        local_grad
        + jnp.dot(one_hot_rows(send_list, pin_count), received, preferred_element_type=F32)
    ).astype(BF16)
    pieces = (self_sum, edge_sum.reshape(-1, feat_width), head_sum_t)
    totals = all_sum(jnp.concatenate(pieces, 0), owners)
    grad_scale = 1.0 / math.sqrt(pin_count * owners)
    outs = []
    offset = 0
    for piece in pieces:
        outs.append(totals[offset : offset + piece.shape[0]] * grad_scale)
        offset += piece.shape[0]
    return (
        predicted,
        grad_feats,
        outs[0],
        outs[1].reshape(edge_sum.shape),
        outs[2].T,
        out_total * grad_scale,
    )


def solution(mesh):
    in_specs = (
        P(ALL, None),
        P(),
        P(),
        P(),
        P(),
        P(ALL, None),
        P(ALL, None, None),
        P(ALL, None, None),
        P(ALL, None),
        P(ALL),
        P(ALL),
    )
    out_specs = (P(ALL), P(ALL, None), P(), P(), P(), P())
    shape = mesh.devices.shape
    cores = 2
    chip_mesh = jax.sharding.Mesh(
        mesh.devices.reshape(shape[0], shape[1] // cores, cores), ("group", "zdom", "core")
    )
    return jax.shard_map(
        on_device, mesh=chip_mesh, in_specs=in_specs, out_specs=out_specs, check_vma=False
    )
```

```python
import math

import jax
import jax.numpy as jnp
from jax import lax
from jax.sharding import PartitionSpec as P


F32 = jnp.float32
BF16 = jnp.bfloat16


DOM = ("zdom", "core")
ALL = ("group",) + DOM
CHIP = ("group", "zdom")


def size_of(axes):
    return math.prod(lax.axis_size(axis) for axis in axes)


def extended(block, sides, width):
    for axis, dim in sides:
        count = size_of(axis)
        forward = [(i, i + 1) for i in range(count - 1)]
        backward = [(target, source) for source, target in forward]
        low = lax.ppermute(
            lax.slice_in_dim(block, block.shape[dim] - width, None, axis=dim), axis, forward
        )
        high = lax.ppermute(lax.slice_in_dim(block, 0, width, axis=dim), axis, backward)
        block = jnp.concatenate([low, block, high], axis=dim)
    return block


def silu_slope(values):
    sigma_val = jax.nn.sigmoid(values)
    return sigma_val * (1.0 + values * (1.0 - sigma_val))


def one_hot(index, count):
    return (index[..., None] == jnp.arange(count, dtype=index.dtype)).astype(BF16)


def one_hot_rows(index, count):
    return (jnp.arange(count, dtype=index.dtype)[:, None] == index[..., None, :]).astype(BF16)


def split_dot(spec, left, right):
    return jnp.einsum(
        spec, left, right.astype(F32), precision=lax.Precision.HIGHEST, preferred_element_type=F32
    )


def all_sum(rows, owners):
    count, width = rows.shape
    chips = size_of(CHIP)
    cores = lax.axis_size("core")
    unit = chips * cores * 8
    length = -(-count // unit) * unit
    rows = jnp.pad(rows, ((0, length - count), (0, 0))).reshape(cores, length // cores, width)
    core = lax.axis_index("core")
    swap = [(i, (i + 1) % cores) for i in range(cores)]
    kept = lax.dynamic_index_in_dim(rows, core, 0, keepdims=False)
    given = lax.dynamic_index_in_dim(rows, (core + 1) % cores, 0, keepdims=False)
    half = kept + lax.ppermute(given.astype(BF16), "core", swap).astype(F32)
    mine = lax.all_to_all(
        half.astype(BF16).reshape(chips, -1, width), CHIP, split_axis=0, concat_axis=0, tiled=True
    )
    mine = jnp.einsum(
        "o,orw->rw", jnp.ones((chips,), BF16), mine, preferred_element_type=F32
    ).astype(BF16)
    spread = jnp.broadcast_to(mine[None], (chips,) + mine.shape)
    own_half = lax.all_to_all(spread, CHIP, split_axis=0, concat_axis=0, tiled=True).reshape(
        -1, width
    )
    other_half = lax.ppermute(own_half, "core", swap)
    first = jnp.where(core == 0, own_half, other_half)
    second = jnp.where(core == 0, other_half, own_half)
    return jnp.concatenate([first, second], 0)[:count].astype(F32)


def on_device(
    pin_feats,
    w_self,
    w_edge,
    w_head,
    w_out,
    send_rows,
    edge_src,
    edge_dst,
    pin_owner,
    pin_net,
    net_target,
):
    pin_count, feat_width = pin_feats.shape
    send_list = send_rows[0]
    halo_span = send_list.shape[0] // 2
    send_hot = one_hot(send_list, pin_count)
    outgoing = jnp.dot(send_hot, pin_feats, preferred_element_type=F32).astype(BF16)
    padded = extended(outgoing, ((DOM, 0),), halo_span)
    node_table = jnp.concatenate([pin_feats, padded[:halo_span], padded[3 * halo_span :]], 0)
    table_rows = node_table.shape[0]
    sources = edge_src[0]
    endpoints = edge_dst[0]
    src_hot = one_hot(sources, table_rows)
    dst_hot = one_hot(endpoints, pin_count)
    gathered = jnp.einsum(
        "ter,rd->ted", src_hot, node_table, preferred_element_type=F32
    ).astype(BF16)
    edge_in = jnp.einsum(
        "tpe,ted->tpd", one_hot_rows(endpoints, pin_count), gathered, preferred_element_type=F32
    )
    summed = split_dot("tpk,tkd->pd", edge_in, w_edge)
    degree = jnp.sum(dst_hot.astype(F32), axis=(0, 1))
    inverse = 1.0 / (1.0 + degree)
    preact = (
        jnp.dot(pin_feats, w_self, preferred_element_type=F32) + summed * inverse[:, None]
    )
    hidden = jax.nn.silu(preact).astype(BF16)
    groups = lax.axis_size("group")
    domains = size_of(DOM)
    owners = groups * domains
    capacity = max(2, 2 * pin_count // owners)
    net_count = net_target.shape[0]
    owner_ids = pin_owner[:, 0]
    owner_hot = one_hot(owner_ids, owners)
    earlier = (
        jnp.arange(pin_count, dtype=jnp.int32)[None, :]
        < jnp.arange(pin_count, dtype=jnp.int32)[:, None]
    ).astype(BF16)
    before = jnp.dot(earlier, owner_hot, preferred_element_type=F32)
    slot_rank = jnp.sum(before * owner_hot.astype(F32), axis=1).astype(jnp.int32)
    pin_slot = owner_ids * capacity + slot_rank
    slot_hot = one_hot(pin_slot, owners * capacity)
    net_code = (pin_net + 1).astype(BF16)[:, None]
    slot_rows = one_hot_rows(pin_slot, owners * capacity)
    slot_nets = jnp.dot(slot_rows, net_code, preferred_element_type=F32)[:, 0] - 1.0
    outbound = jnp.dot(slot_rows, hidden, preferred_element_type=F32).astype(BF16)
    id_rows = -(-capacity // (8 * feat_width)) * 8
    id_block = jnp.pad(
        slot_nets.reshape(owners, capacity), ((0, 0), (0, id_rows * feat_width - capacity))
    ).astype(BF16)
    packet = jnp.concatenate(
        [
            outbound.reshape(owners, capacity, feat_width),
            id_block.reshape(owners, id_rows, feat_width),
        ],
        1,
    )
    packet_in = lax.all_to_all(packet, ALL, split_axis=0, concat_axis=0, tiled=True)
    inbound = packet_in[:, :capacity].reshape(-1, feat_width)
    slot_nets_in = (
        packet_in[:, capacity:].reshape(owners, -1)[:, :capacity].astype(F32).astype(jnp.int32)
    ).reshape(-1)
    net_hot = one_hot(slot_nets_in, net_count)
    pooled = jnp.dot(
        one_hot_rows(slot_nets_in, net_count), inbound, preferred_element_type=F32
    )
    pooled_b = pooled.astype(BF16)
    head_pre = jnp.dot(pooled_b, w_head, preferred_element_type=F32)
    activated = jax.nn.silu(head_pre).astype(BF16)
    predicted = jnp.dot(activated, w_out, preferred_element_type=F32)
    misfit = predicted - net_target
    head_grad = (
        misfit[:, None] * w_out.astype(F32)[None, :] * silu_slope(head_pre)
    ).astype(BF16)
    head_sum_t = jnp.einsum("nh,nd->hd", head_grad, pooled_b, preferred_element_type=F32)
    out_sum = jnp.dot(misfit, activated.astype(F32), precision=lax.Precision.HIGHEST)
    net_grad = jnp.einsum(
        "nh,dh->nd", head_grad, w_head, preferred_element_type=F32
    ).astype(BF16)
    returned = jnp.dot(net_hot, net_grad, preferred_element_type=F32).astype(BF16)
    out_rows = out_sum.reshape(-1, feat_width).astype(BF16)
    back_rows = -(-(capacity + out_rows.shape[0]) // 8) * 8
    back_packet = jnp.concatenate(
        [
            returned.reshape(owners, capacity, feat_width),
            jnp.broadcast_to(out_rows[None], (owners,) + out_rows.shape),
            jnp.zeros(
                (owners, back_rows - capacity - out_rows.shape[0], feat_width), BF16
            ),
        ],
        1,
    )
    back_in = lax.all_to_all(
        back_packet, ALL, split_axis=0, concat_axis=0, tiled=True
    )
    arrived = back_in[:, :capacity].reshape(-1, feat_width)
    out_total = jnp.einsum(
        "o,orw->rw",
        jnp.ones((owners,), BF16),
        back_in[:, capacity : capacity + out_rows.shape[0]],
        preferred_element_type=F32,
    ).reshape(-1)
    pin_grad = jnp.dot(slot_hot, arrived, preferred_element_type=F32)
    preact_grad = (pin_grad * silu_slope(preact)).astype(BF16)
    self_sum = jnp.einsum("pk,pd->kd", pin_feats, preact_grad, preferred_element_type=F32)
    agg_grad = (preact_grad.astype(F32) * inverse[:, None]).astype(BF16)
    edge_rows = jnp.einsum(
        "tep,pd->ted", dst_hot, agg_grad, preferred_element_type=F32
    ).astype(BF16)
    edge_sum = jnp.einsum("tek,ted->tkd", gathered, edge_rows, preferred_element_type=F32)
    row_in = jnp.einsum(
        "tre,ted->trd", one_hot_rows(sources, table_rows), edge_rows, preferred_element_type=F32
    )
    table_grad = split_dot("trd,tkd->rk", row_in, w_edge)
    local_grad = (
        jnp.einsum("pd,kd->pk", preact_grad, w_self, preferred_element_type=F32)
        + table_grad[:pin_count]
    )
    halo_grad = table_grad[pin_count:].astype(BF16)
    back_padded = extended(halo_grad, ((DOM, 0),), halo_span)
    received = jnp.concatenate([back_padded[:halo_span], back_padded[3 * halo_span :]], 0)
    grad_feats = (
        local_grad
        + jnp.dot(one_hot_rows(send_list, pin_count), received, preferred_element_type=F32)
    ).astype(BF16)
    pieces = (self_sum, edge_sum.reshape(-1, feat_width), head_sum_t)
    totals = all_sum(jnp.concatenate(pieces, 0), owners)
    grad_scale = 1.0 / math.sqrt(pin_count * owners)
    outs = []
    offset = 0
    for piece in pieces:
        outs.append(totals[offset : offset + piece.shape[0]] * grad_scale)
        offset += piece.shape[0]
    return (
        predicted,
        grad_feats,
        outs[0],
        outs[1].reshape(edge_sum.shape),
        outs[2].T,
        out_total * grad_scale,
    )


def solution(mesh):
    in_specs = (
        P(ALL, None),
        P(),
        P(),
        P(),
        P(),
        P(ALL, None),
        P(ALL, None, None),
        P(ALL, None, None),
        P(ALL, None),
        P(ALL),
        P(ALL),
    )
    out_specs = (P(ALL), P(ALL, None), P(), P(), P(), P())
    shape = mesh.devices.shape
    cores = 2
    chip_mesh = jax.sharding.Mesh(
        mesh.devices.reshape(shape[0], shape[1] // cores, cores), ("group", "zdom", "core")
    )
    return jax.shard_map(
        on_device, mesh=chip_mesh, in_specs=in_specs, out_specs=out_specs, check_vma=False
    )
```

```python
import math

import jax
import jax.numpy as jnp
from jax import lax
from jax.sharding import PartitionSpec as P


F32 = jnp.float32
BF16 = jnp.bfloat16


DOM = ("zdom", "core")
ALL = ("group",) + DOM
CHIP = ("group", "zdom")


def size_of(axes):
    return math.prod(lax.axis_size(axis) for axis in axes)


def extended(block, sides, width):
    for axis, dim in sides:
        count = size_of(axis)
        forward = [(i, i + 1) for i in range(count - 1)]
        backward = [(target, source) for source, target in forward]
        low = lax.ppermute(
            lax.slice_in_dim(block, block.shape[dim] - width, None, axis=dim), axis, forward
        )
        high = lax.ppermute(lax.slice_in_dim(block, 0, width, axis=dim), axis, backward)
        block = jnp.concatenate([low, block, high], axis=dim)
    return block


def silu_slope(values):
    sigma_val = jax.nn.sigmoid(values)
    return sigma_val * (1.0 + values * (1.0 - sigma_val))


def one_hot(index, count):
    return (index[..., None] == jnp.arange(count, dtype=index.dtype)).astype(BF16)


def one_hot_rows(index, count):
    return (jnp.arange(count, dtype=index.dtype)[:, None] == index[..., None, :]).astype(BF16)


def split_dot(spec, left, right):
    return jnp.einsum(
        spec, left, right.astype(F32), precision=lax.Precision.HIGHEST, preferred_element_type=F32
    )


def all_sum(rows, owners):
    count, width = rows.shape
    chips = size_of(CHIP)
    cores = lax.axis_size("core")
    unit = chips * cores * 8
    length = -(-count // unit) * unit
    rows = jnp.pad(rows, ((0, length - count), (0, 0))).reshape(cores, length // cores, width)
    core = lax.axis_index("core")
    swap = [(i, (i + 1) % cores) for i in range(cores)]
    kept = lax.dynamic_index_in_dim(rows, core, 0, keepdims=False)
    given = lax.dynamic_index_in_dim(rows, (core + 1) % cores, 0, keepdims=False)
    half = kept + lax.ppermute(given.astype(BF16), "core", swap).astype(F32)
    mine = lax.all_to_all(
        half.astype(BF16).reshape(chips, -1, width), CHIP, split_axis=0, concat_axis=0, tiled=True
    )
    mine = jnp.einsum(
        "o,orw->rw", jnp.ones((chips,), BF16), mine, preferred_element_type=F32
    ).astype(BF16)
    spread = jnp.broadcast_to(mine[None], (chips,) + mine.shape)
    own_half = lax.all_to_all(spread, CHIP, split_axis=0, concat_axis=0, tiled=True).reshape(
        -1, width
    )
    other_half = lax.ppermute(own_half, "core", swap)
    first = jnp.where(core == 0, own_half, other_half)
    second = jnp.where(core == 0, other_half, own_half)
    return jnp.concatenate([first, second], 0)[:count].astype(F32)


def on_device(
    pin_feats,
    w_self,
    w_edge,
    w_head,
    w_out,
    send_rows,
    edge_src,
    edge_dst,
    pin_owner,
    pin_net,
    net_target,
):
    pin_count, feat_width = pin_feats.shape
    send_list = send_rows[0]
    halo_span = send_list.shape[0] // 2
    send_hot = one_hot(send_list, pin_count)
    outgoing = jnp.dot(send_hot, pin_feats, preferred_element_type=F32).astype(BF16)
    padded = extended(outgoing, ((DOM, 0),), halo_span)
    node_table = jnp.concatenate([pin_feats, padded[:halo_span], padded[3 * halo_span :]], 0)
    table_rows = node_table.shape[0]
    sources = edge_src[0]
    endpoints = edge_dst[0]
    src_hot = one_hot(sources, table_rows)
    dst_hot = one_hot(endpoints, pin_count)
    gathered = jnp.einsum(
        "ter,rd->ted", src_hot, node_table, preferred_element_type=F32
    ).astype(BF16)
    edge_in = jnp.einsum(
        "tpe,ted->tpd", one_hot_rows(endpoints, pin_count), gathered, preferred_element_type=F32
    )
    summed = split_dot("tpk,tkd->pd", edge_in, w_edge)
    degree = jnp.sum(dst_hot.astype(F32), axis=(0, 1))
    inverse = 1.0 / (1.0 + degree)
    preact = (
        jnp.dot(pin_feats, w_self, preferred_element_type=F32) + summed * inverse[:, None]
    )
    hidden = jax.nn.silu(preact).astype(BF16)
    groups = lax.axis_size("group")
    domains = size_of(DOM)
    owners = groups * domains
    capacity = max(2, 2 * pin_count // owners)
    net_count = net_target.shape[0]
    owner_ids = pin_owner[:, 0]
    owner_hot = one_hot(owner_ids, owners)
    earlier = (
        jnp.arange(pin_count, dtype=jnp.int32)[None, :]
        < jnp.arange(pin_count, dtype=jnp.int32)[:, None]
    ).astype(BF16)
    before = jnp.dot(earlier, owner_hot, preferred_element_type=F32)
    slot_rank = jnp.sum(before * owner_hot.astype(F32), axis=1).astype(jnp.int32)
    pin_slot = owner_ids * capacity + slot_rank
    slot_hot = one_hot(pin_slot, owners * capacity)
    net_code = (pin_net + 1).astype(BF16)[:, None]
    slot_rows = one_hot_rows(pin_slot, owners * capacity)
    slot_nets = jnp.dot(slot_rows, net_code, preferred_element_type=F32)[:, 0] - 1.0
    outbound = jnp.dot(slot_rows, hidden, preferred_element_type=F32).astype(BF16)
    id_rows = -(-capacity // (8 * feat_width)) * 8
    id_block = jnp.pad(
        slot_nets.reshape(owners, capacity), ((0, 0), (0, id_rows * feat_width - capacity))
    ).astype(BF16)
    packet = jnp.concatenate(
        [
            outbound.reshape(owners, capacity, feat_width),
            id_block.reshape(owners, id_rows, feat_width),
        ],
        1,
    )
    packet_in = lax.all_to_all(packet, ALL, split_axis=0, concat_axis=0, tiled=True)
    inbound = packet_in[:, :capacity].reshape(-1, feat_width)
    slot_nets_in = (
        packet_in[:, capacity:].reshape(owners, -1)[:, :capacity].astype(F32).astype(jnp.int32)
    ).reshape(-1)
    net_hot = one_hot(slot_nets_in, net_count)
    slot_hot, dst_hot, inbound = lax.optimization_barrier((slot_hot, dst_hot, inbound))
    pooled = jnp.dot(
        one_hot_rows(slot_nets_in, net_count), inbound, preferred_element_type=F32
    )
    pooled_b = pooled.astype(BF16)
    head_pre = jnp.dot(pooled_b, w_head, preferred_element_type=F32)
    activated = jax.nn.silu(head_pre).astype(BF16)
    predicted = jnp.dot(activated, w_out, preferred_element_type=F32)
    misfit = predicted - net_target
    head_grad = (
        misfit[:, None] * w_out.astype(F32)[None, :] * silu_slope(head_pre)
    ).astype(BF16)
    head_sum_t = jnp.einsum("nh,nd->hd", head_grad, pooled_b, preferred_element_type=F32)
    out_sum = jnp.dot(misfit, activated.astype(F32), precision=lax.Precision.HIGHEST)
    net_grad = jnp.einsum(
        "nh,dh->nd", head_grad, w_head, preferred_element_type=F32
    ).astype(BF16)
    returned = jnp.dot(net_hot, net_grad, preferred_element_type=F32).astype(BF16)
    out_rows = out_sum.reshape(-1, feat_width).astype(BF16)
    back_rows = -(-(capacity + out_rows.shape[0]) // 8) * 8
    back_packet = jnp.concatenate(
        [
            returned.reshape(owners, capacity, feat_width),
            jnp.broadcast_to(out_rows[None], (owners,) + out_rows.shape),
            jnp.zeros(
                (owners, back_rows - capacity - out_rows.shape[0], feat_width), BF16
            ),
        ],
        1,
    )
    back_in = lax.all_to_all(
        back_packet, ALL, split_axis=0, concat_axis=0, tiled=True
    )
    arrived = back_in[:, :capacity].reshape(-1, feat_width)
    out_total = jnp.einsum(
        "o,orw->rw",
        jnp.ones((owners,), BF16),
        back_in[:, capacity : capacity + out_rows.shape[0]],
        preferred_element_type=F32,
    ).reshape(-1)
    pin_grad = jnp.dot(slot_hot, arrived, preferred_element_type=F32)
    preact_grad = (pin_grad * silu_slope(preact)).astype(BF16)
    self_sum = jnp.einsum("pk,pd->kd", pin_feats, preact_grad, preferred_element_type=F32)
    agg_grad = (preact_grad.astype(F32) * inverse[:, None]).astype(BF16)
    edge_rows = jnp.einsum(
        "tep,pd->ted", dst_hot, agg_grad, preferred_element_type=F32
    ).astype(BF16)
    edge_sum = jnp.einsum("tek,ted->tkd", gathered, edge_rows, preferred_element_type=F32)
    row_in = jnp.einsum(
        "tre,ted->trd", one_hot_rows(sources, table_rows), edge_rows, preferred_element_type=F32
    )
    table_grad = split_dot("trd,tkd->rk", row_in, w_edge)
    local_grad = (
        jnp.einsum("pd,kd->pk", preact_grad, w_self, preferred_element_type=F32)
        + table_grad[:pin_count]
    )
    halo_grad = table_grad[pin_count:].astype(BF16)
    back_padded = extended(halo_grad, ((DOM, 0),), halo_span)
    received = jnp.concatenate([back_padded[:halo_span], back_padded[3 * halo_span :]], 0)
    grad_feats = (
        local_grad
        + jnp.dot(one_hot_rows(send_list, pin_count), received, preferred_element_type=F32)
    ).astype(BF16)
    pieces = (self_sum, edge_sum.reshape(-1, feat_width), head_sum_t)
    totals = all_sum(jnp.concatenate(pieces, 0), owners)
    grad_scale = 1.0 / math.sqrt(pin_count * owners)
    outs = []
    offset = 0
    for piece in pieces:
        outs.append(totals[offset : offset + piece.shape[0]] * grad_scale)
        offset += piece.shape[0]
    return (
        predicted,
        grad_feats,
        outs[0],
        outs[1].reshape(edge_sum.shape),
        outs[2].T,
        out_total * grad_scale,
    )


def solution(mesh):
    in_specs = (
        P(ALL, None),
        P(),
        P(),
        P(),
        P(),
        P(ALL, None),
        P(ALL, None, None),
        P(ALL, None, None),
        P(ALL, None),
        P(ALL),
        P(ALL),
    )
    out_specs = (P(ALL), P(ALL, None), P(), P(), P(), P())
    shape = mesh.devices.shape
    cores = 2
    chip_mesh = jax.sharding.Mesh(
        mesh.devices.reshape(shape[0], shape[1] // cores, cores), ("group", "zdom", "core")
    )
    return jax.shard_map(
        on_device, mesh=chip_mesh, in_specs=in_specs, out_specs=out_specs, check_vma=False
    )
```

```python
import math

import jax
import jax.numpy as jnp
from jax import lax
from jax.sharding import PartitionSpec as P


F32 = jnp.float32
BF16 = jnp.bfloat16


DOM = ("zdom", "core")
ALL = ("group",) + DOM
CHIP = ("group", "zdom")


def size_of(axes):
    return math.prod(lax.axis_size(axis) for axis in axes)


def extended(block, sides, width):
    for axis, dim in sides:
        count = size_of(axis)
        forward = [(i, i + 1) for i in range(count - 1)]
        backward = [(target, source) for source, target in forward]
        low = lax.ppermute(
            lax.slice_in_dim(block, block.shape[dim] - width, None, axis=dim), axis, forward
        )
        high = lax.ppermute(lax.slice_in_dim(block, 0, width, axis=dim), axis, backward)
        block = jnp.concatenate([low, block, high], axis=dim)
    return block


def silu_slope(values):
    sigma_val = jax.nn.sigmoid(values)
    return sigma_val * (1.0 + values * (1.0 - sigma_val))


def one_hot(index, count):
    return (index[..., None] == jnp.arange(count, dtype=index.dtype)).astype(BF16)


def one_hot_rows(index, count):
    return (jnp.arange(count, dtype=index.dtype)[:, None] == index[..., None, :]).astype(BF16)


def split_dot(spec, left, right):
    return jnp.einsum(
        spec, left, right.astype(F32), precision=lax.Precision.HIGHEST, preferred_element_type=F32
    )


def all_sum(rows, owners):
    count, width = rows.shape
    chips = size_of(CHIP)
    cores = lax.axis_size("core")
    unit = chips * cores * 8
    length = -(-count // unit) * unit
    rows = jnp.pad(rows, ((0, length - count), (0, 0))).reshape(cores, length // cores, width)
    core = lax.axis_index("core")
    swap = [(i, (i + 1) % cores) for i in range(cores)]
    kept = lax.dynamic_index_in_dim(rows, core, 0, keepdims=False)
    given = lax.dynamic_index_in_dim(rows, (core + 1) % cores, 0, keepdims=False)
    half = kept + lax.ppermute(given.astype(BF16), "core", swap).astype(F32)
    mine = lax.all_to_all(
        half.astype(BF16).reshape(chips, -1, width), CHIP, split_axis=0, concat_axis=0, tiled=True
    )
    mine = jnp.einsum(
        "o,orw->rw", jnp.ones((chips,), BF16), mine, preferred_element_type=F32
    ).astype(BF16)
    spread = jnp.broadcast_to(mine[None], (chips,) + mine.shape)
    own_half = lax.all_to_all(spread, CHIP, split_axis=0, concat_axis=0, tiled=True).reshape(
        -1, width
    )
    other_half = lax.ppermute(own_half, "core", swap)
    first = jnp.where(core == 0, own_half, other_half)
    second = jnp.where(core == 0, other_half, own_half)
    return jnp.concatenate([first, second], 0)[:count].astype(F32)


def on_device(
    pin_feats,
    w_self,
    w_edge,
    w_head,
    w_out,
    send_rows,
    edge_src,
    edge_dst,
    pin_owner,
    pin_net,
    net_target,
):
    pin_count, feat_width = pin_feats.shape
    send_list = send_rows[0]
    halo_span = send_list.shape[0] // 2
    send_hot = one_hot(send_list, pin_count)
    outgoing = jnp.dot(send_hot, pin_feats, preferred_element_type=F32).astype(BF16)
    padded = extended(outgoing, ((DOM, 0),), halo_span)
    node_table = jnp.concatenate([pin_feats, padded[:halo_span], padded[3 * halo_span :]], 0)
    table_rows = node_table.shape[0]
    sources = edge_src[0]
    endpoints = edge_dst[0]
    src_hot = one_hot(sources, table_rows)
    dst_hot = one_hot(endpoints, pin_count)
    gathered = jnp.einsum(
        "ter,rd->ted", src_hot, node_table, preferred_element_type=F32
    ).astype(BF16)
    edge_in = jnp.einsum(
        "tpe,ted->tpd", one_hot_rows(endpoints, pin_count), gathered, preferred_element_type=F32
    )
    summed = split_dot("tpk,tkd->pd", edge_in, w_edge)
    degree = jnp.sum(dst_hot.astype(F32), axis=(0, 1))
    inverse = 1.0 / (1.0 + degree)
    preact = (
        jnp.dot(pin_feats, w_self, preferred_element_type=F32) + summed * inverse[:, None]
    )
    hidden = jax.nn.silu(preact).astype(BF16)
    groups = lax.axis_size("group")
    domains = size_of(DOM)
    owners = groups * domains
    capacity = max(2, 2 * pin_count // owners)
    net_count = net_target.shape[0]
    owner_ids = pin_owner[:, 0]
    owner_hot = one_hot(owner_ids, owners)
    earlier = (
        jnp.arange(pin_count, dtype=jnp.int32)[None, :]
        < jnp.arange(pin_count, dtype=jnp.int32)[:, None]
    ).astype(BF16)
    before = jnp.dot(earlier, owner_hot, preferred_element_type=F32)
    slot_rank = jnp.sum(before * owner_hot.astype(F32), axis=1).astype(jnp.int32)
    pin_slot = owner_ids * capacity + slot_rank
    slot_hot = one_hot(pin_slot, owners * capacity)
    net_code = (pin_net + 1).astype(BF16)[:, None]
    slot_rows = one_hot_rows(pin_slot, owners * capacity)
    slot_nets = jnp.dot(slot_rows, net_code, preferred_element_type=F32)[:, 0] - 1.0
    outbound = jnp.dot(slot_rows, hidden, preferred_element_type=F32).astype(BF16)
    id_rows = -(-capacity // (8 * feat_width)) * 8
    id_block = jnp.pad(
        slot_nets.reshape(owners, capacity), ((0, 0), (0, id_rows * feat_width - capacity))
    ).astype(BF16)
    packet = jnp.concatenate(
        [
            outbound.reshape(owners, capacity, feat_width),
            id_block.reshape(owners, id_rows, feat_width),
        ],
        1,
    )
    packet_in = lax.all_to_all(packet, ALL, split_axis=0, concat_axis=0, tiled=True)
    inbound = packet_in[:, :capacity].reshape(-1, feat_width)
    slot_nets_in = (
        packet_in[:, capacity:].reshape(owners, -1)[:, :capacity].astype(F32).astype(jnp.int32)
    ).reshape(-1)
    net_hot = one_hot(slot_nets_in, net_count)
    pooled = jnp.dot(
        one_hot_rows(slot_nets_in, net_count), inbound, preferred_element_type=F32
    )
    pooled_b = pooled.astype(BF16)
    head_pre = jnp.dot(pooled_b, w_head, preferred_element_type=F32)
    activated = jax.nn.silu(head_pre).astype(BF16)
    predicted = jnp.dot(activated, w_out, preferred_element_type=F32)
    misfit = predicted - net_target
    head_grad = (
        misfit[:, None] * w_out.astype(F32)[None, :] * silu_slope(head_pre)
    ).astype(BF16)
    head_sum_t = jnp.einsum("nh,nd->hd", head_grad, pooled_b, preferred_element_type=F32)
    out_sum = jnp.dot(misfit, activated.astype(F32), precision=lax.Precision.HIGHEST)
    net_grad = jnp.einsum(
        "nh,dh->nd", head_grad, w_head, preferred_element_type=F32
    ).astype(BF16)
    returned = jnp.dot(net_hot, net_grad, preferred_element_type=F32).astype(BF16)
    out_rows = (out_sum * (1.0 / math.sqrt(pin_count * owners))).reshape(-1, feat_width).astype(BF16)
    back_rows = -(-(capacity + out_rows.shape[0]) // 8) * 8
    back_packet = jnp.concatenate(
        [
            returned.reshape(owners, capacity, feat_width),
            jnp.broadcast_to(out_rows[None], (owners,) + out_rows.shape),
            jnp.zeros(
                (owners, back_rows - capacity - out_rows.shape[0], feat_width), BF16
            ),
        ],
        1,
    )
    back_in = lax.all_to_all(
        back_packet, ALL, split_axis=0, concat_axis=0, tiled=True
    )
    arrived = back_in[:, :capacity].reshape(-1, feat_width)
    out_total = jnp.einsum(
        "o,orw->rw",
        jnp.ones((owners,), BF16),
        back_in[:, capacity : capacity + out_rows.shape[0]],
        preferred_element_type=F32,
    ).reshape(-1)
    pin_grad = jnp.dot(slot_hot, arrived, preferred_element_type=F32)
    preact_grad = (pin_grad * silu_slope(preact)).astype(BF16)
    self_sum = jnp.einsum("pk,pd->kd", pin_feats, preact_grad, preferred_element_type=F32)
    agg_grad = (preact_grad.astype(F32) * inverse[:, None]).astype(BF16)
    edge_rows = jnp.einsum(
        "tep,pd->ted", dst_hot, agg_grad, preferred_element_type=F32
    ).astype(BF16)
    edge_sum = jnp.einsum("tek,ted->tkd", gathered, edge_rows, preferred_element_type=F32)
    row_in = jnp.einsum(
        "tre,ted->trd", one_hot_rows(sources, table_rows), edge_rows, preferred_element_type=F32
    )
    table_grad = split_dot("trd,tkd->rk", row_in, w_edge)
    local_grad = (
        jnp.einsum("pd,kd->pk", preact_grad, w_self, preferred_element_type=F32)
        + table_grad[:pin_count]
    )
    halo_grad = table_grad[pin_count:].astype(BF16)
    back_padded = extended(halo_grad, ((DOM, 0),), halo_span)
    received = jnp.concatenate([back_padded[:halo_span], back_padded[3 * halo_span :]], 0)
    grad_feats = (
        local_grad
        + jnp.dot(one_hot_rows(send_list, pin_count), received, preferred_element_type=F32)
    ).astype(BF16)
    grad_scale = 1.0 / math.sqrt(pin_count * owners)
    pieces = (self_sum, edge_sum.reshape(-1, feat_width), head_sum_t)
    totals = all_sum(jnp.concatenate(pieces, 0) * grad_scale, owners)
    outs = []
    offset = 0
    for piece in pieces:
        outs.append(totals[offset : offset + piece.shape[0]])
        offset += piece.shape[0]
    return (
        predicted,
        grad_feats,
        outs[0],
        outs[1].reshape(edge_sum.shape),
        outs[2].T,
        out_total,
    )


def solution(mesh):
    in_specs = (
        P(ALL, None),
        P(),
        P(),
        P(),
        P(),
        P(ALL, None),
        P(ALL, None, None),
        P(ALL, None, None),
        P(ALL, None),
        P(ALL),
        P(ALL),
    )
    out_specs = (P(ALL), P(ALL, None), P(), P(), P(), P())
    shape = mesh.devices.shape
    cores = 2
    chip_mesh = jax.sharding.Mesh(
        mesh.devices.reshape(shape[0], shape[1] // cores, cores), ("group", "zdom", "core")
    )
    return jax.shard_map(
        on_device, mesh=chip_mesh, in_specs=in_specs, out_specs=out_specs, check_vma=False
    )
```

```python
import math

import jax
import jax.numpy as jnp
from jax import lax
from jax.sharding import PartitionSpec as P


F32 = jnp.float32
BF16 = jnp.bfloat16


DOM = ("zdom", "core")
ALL = ("group",) + DOM
CHIP = ("group", "zdom")


def size_of(axes):
    return math.prod(lax.axis_size(axis) for axis in axes)


def extended(block, sides, width):
    for axis, dim in sides:
        count = size_of(axis)
        forward = [(i, i + 1) for i in range(count - 1)]
        backward = [(target, source) for source, target in forward]
        low = lax.ppermute(
            lax.slice_in_dim(block, block.shape[dim] - width, None, axis=dim), axis, forward
        )
        high = lax.ppermute(lax.slice_in_dim(block, 0, width, axis=dim), axis, backward)
        block = jnp.concatenate([low, block, high], axis=dim)
    return block


def silu_slope(values):
    sigma_val = jax.nn.sigmoid(values)
    return sigma_val * (1.0 + values * (1.0 - sigma_val))


def one_hot(index, count):
    return (index[..., None] == jnp.arange(count, dtype=index.dtype)).astype(BF16)


def one_hot_rows(index, count):
    return (jnp.arange(count, dtype=index.dtype)[:, None] == index[..., None, :]).astype(BF16)


def split_dot(spec, left, right):
    return jnp.einsum(
        spec, left, right.astype(F32), precision=lax.Precision.HIGHEST, preferred_element_type=F32
    )


def all_sum(rows, owners):
    count, width = rows.shape
    chips = size_of(CHIP)
    cores = lax.axis_size("core")
    unit = chips * cores * 8
    length = -(-count // unit) * unit
    rows = jnp.pad(rows, ((0, length - count), (0, 0))).reshape(cores, length // cores, width)
    core = lax.axis_index("core")
    swap = [(i, (i + 1) % cores) for i in range(cores)]
    kept = lax.dynamic_index_in_dim(rows, core, 0, keepdims=False)
    given = lax.dynamic_index_in_dim(rows, (core + 1) % cores, 0, keepdims=False)
    half = kept + lax.ppermute(given.astype(BF16), "core", swap).astype(F32)
    mine = lax.all_to_all(
        half.astype(BF16).reshape(chips, -1, width), CHIP, split_axis=0, concat_axis=0, tiled=True
    )
    mine = jnp.einsum(
        "o,orw->rw", jnp.ones((chips,), BF16), mine, preferred_element_type=F32
    ).astype(BF16)
    spread = jnp.broadcast_to(mine[None], (chips,) + mine.shape)
    own_half = lax.all_to_all(spread, CHIP, split_axis=0, concat_axis=0, tiled=True).reshape(
        -1, width
    )
    other_half = lax.ppermute(own_half, "core", swap)
    first = jnp.where(core == 0, own_half, other_half)
    second = jnp.where(core == 0, other_half, own_half)
    return jnp.concatenate([first, second], 0)[:count].astype(F32)


def on_device(
    pin_feats,
    w_self,
    w_edge,
    w_head,
    w_out,
    send_rows,
    edge_src,
    edge_dst,
    pin_owner,
    pin_net,
    net_target,
):
    pin_count, feat_width = pin_feats.shape
    send_list = send_rows[0]
    halo_span = send_list.shape[0] // 2
    send_hot = one_hot(send_list, pin_count)
    outgoing = jnp.dot(send_hot, pin_feats, preferred_element_type=F32).astype(BF16)
    padded = extended(outgoing, ((DOM, 0),), halo_span)
    node_table = jnp.concatenate([pin_feats, padded[:halo_span], padded[3 * halo_span :]], 0)
    table_rows = node_table.shape[0]
    sources = edge_src[0]
    endpoints = edge_dst[0]
    src_hot = one_hot(sources, table_rows)
    dst_hot = one_hot(endpoints, pin_count)
    gathered = jnp.einsum(
        "ter,rd->ted", src_hot, node_table, preferred_element_type=F32
    ).astype(BF16)
    edge_in = jnp.einsum(
        "tpe,ted->tpd", one_hot_rows(endpoints, pin_count), gathered, preferred_element_type=F32
    )
    summed = split_dot("tpk,tkd->pd", edge_in, w_edge)
    degree = jnp.sum(dst_hot.astype(F32), axis=(0, 1))
    inverse = 1.0 / (1.0 + degree)
    preact = (
        jnp.dot(pin_feats, w_self, preferred_element_type=F32) + summed * inverse[:, None]
    )
    hidden = jax.nn.silu(preact).astype(BF16)
    groups = lax.axis_size("group")
    domains = size_of(DOM)
    owners = groups * domains
    capacity = max(2, 2 * pin_count // owners)
    net_count = net_target.shape[0]
    owner_ids = pin_owner[:, 0]
    owner_hot = one_hot(owner_ids, owners)
    earlier = (
        jnp.arange(pin_count, dtype=jnp.int32)[None, :]
        < jnp.arange(pin_count, dtype=jnp.int32)[:, None]
    ).astype(BF16)
    before = jnp.dot(earlier, owner_hot, preferred_element_type=F32)
    slot_rank = jnp.sum(before * owner_hot.astype(F32), axis=1).astype(jnp.int32)
    pin_slot = owner_ids * capacity + slot_rank
    slot_hot = one_hot(pin_slot, owners * capacity)
    net_code = jnp.pad((pin_net + 1).astype(BF16)[:, None], ((0, 0), (0, 127)))
    slot_rows = one_hot_rows(pin_slot, owners * capacity)
    routed = jnp.dot(
        slot_rows, jnp.concatenate([hidden, net_code], 1), preferred_element_type=F32
    )
    slot_nets = routed[:, feat_width] - 1.0
    outbound = routed[:, :feat_width].astype(BF16)
    id_rows = -(-capacity // (8 * feat_width)) * 8
    id_block = jnp.pad(
        slot_nets.reshape(owners, capacity), ((0, 0), (0, id_rows * feat_width - capacity))
    ).astype(BF16)
    packet = jnp.concatenate(
        [
            outbound.reshape(owners, capacity, feat_width),
            id_block.reshape(owners, id_rows, feat_width),
        ],
        1,
    )
    packet_in = lax.all_to_all(packet, ALL, split_axis=0, concat_axis=0, tiled=True)
    inbound = packet_in[:, :capacity].reshape(-1, feat_width)
    slot_nets_in = (
        packet_in[:, capacity:].reshape(owners, -1)[:, :capacity].astype(F32).astype(jnp.int32)
    ).reshape(-1)
    net_hot = one_hot(slot_nets_in, net_count)
    pooled = jnp.dot(
        one_hot_rows(slot_nets_in, net_count), inbound, preferred_element_type=F32
    )
    pooled_b = pooled.astype(BF16)
    head_pre = jnp.dot(pooled_b, w_head, preferred_element_type=F32)
    activated = jax.nn.silu(head_pre).astype(BF16)
    predicted = jnp.dot(activated, w_out, preferred_element_type=F32)
    misfit = predicted - net_target
    head_grad = (
        misfit[:, None] * w_out.astype(F32)[None, :] * silu_slope(head_pre)
    ).astype(BF16)
    head_sum_t = jnp.einsum("nh,nd->hd", head_grad, pooled_b, preferred_element_type=F32)
    out_sum = jnp.dot(misfit, activated.astype(F32), precision=lax.Precision.HIGHEST)
    net_grad = jnp.einsum(
        "nh,dh->nd", head_grad, w_head, preferred_element_type=F32
    ).astype(BF16)
    returned = jnp.dot(net_hot, net_grad, preferred_element_type=F32).astype(BF16)
    out_rows = out_sum.reshape(-1, feat_width).astype(BF16)
    back_rows = -(-(capacity + out_rows.shape[0]) // 8) * 8
    back_packet = jnp.concatenate(
        [
            returned.reshape(owners, capacity, feat_width),
            jnp.broadcast_to(out_rows[None], (owners,) + out_rows.shape),
            jnp.zeros(
                (owners, back_rows - capacity - out_rows.shape[0], feat_width), BF16
            ),
        ],
        1,
    )
    back_in = lax.all_to_all(
        back_packet, ALL, split_axis=0, concat_axis=0, tiled=True
    )
    arrived = back_in[:, :capacity].reshape(-1, feat_width)
    out_total = jnp.einsum(
        "o,orw->rw",
        jnp.ones((owners,), BF16),
        back_in[:, capacity : capacity + out_rows.shape[0]],
        preferred_element_type=F32,
    ).reshape(-1)
    pin_grad = jnp.dot(slot_hot, arrived, preferred_element_type=F32)
    preact_grad = (pin_grad * silu_slope(preact)).astype(BF16)
    self_sum = jnp.einsum("pk,pd->kd", pin_feats, preact_grad, preferred_element_type=F32)
    agg_grad = (preact_grad.astype(F32) * inverse[:, None]).astype(BF16)
    edge_rows = jnp.einsum(
        "tep,pd->ted", dst_hot, agg_grad, preferred_element_type=F32
    ).astype(BF16)
    edge_sum = jnp.einsum("tek,ted->tkd", gathered, edge_rows, preferred_element_type=F32)
    row_in = jnp.einsum(
        "tre,ted->trd", one_hot_rows(sources, table_rows), edge_rows, preferred_element_type=F32
    )
    table_grad = split_dot("trd,tkd->rk", row_in, w_edge)
    local_grad = (
        jnp.einsum("pd,kd->pk", preact_grad, w_self, preferred_element_type=F32)
        + table_grad[:pin_count]
    )
    halo_grad = table_grad[pin_count:].astype(BF16)
    back_padded = extended(halo_grad, ((DOM, 0),), halo_span)
    received = jnp.concatenate([back_padded[:halo_span], back_padded[3 * halo_span :]], 0)
    grad_feats = (
        local_grad
        + jnp.dot(one_hot_rows(send_list, pin_count), received, preferred_element_type=F32)
    ).astype(BF16)
    pieces = (self_sum, edge_sum.reshape(-1, feat_width), head_sum_t)
    totals = all_sum(jnp.concatenate(pieces, 0), owners)
    grad_scale = 1.0 / math.sqrt(pin_count * owners)
    outs = []
    offset = 0
    for piece in pieces:
        outs.append(totals[offset : offset + piece.shape[0]] * grad_scale)
        offset += piece.shape[0]
    return (
        predicted,
        grad_feats,
        outs[0],
        outs[1].reshape(edge_sum.shape),
        outs[2].T,
        out_total * grad_scale,
    )


def solution(mesh):
    in_specs = (
        P(ALL, None),
        P(),
        P(),
        P(),
        P(),
        P(ALL, None),
        P(ALL, None, None),
        P(ALL, None, None),
        P(ALL, None),
        P(ALL),
        P(ALL),
    )
    out_specs = (P(ALL), P(ALL, None), P(), P(), P(), P())
    shape = mesh.devices.shape
    cores = 2
    chip_mesh = jax.sharding.Mesh(
        mesh.devices.reshape(shape[0], shape[1] // cores, cores), ("group", "zdom", "core")
    )
    return jax.shard_map(
        on_device, mesh=chip_mesh, in_specs=in_specs, out_specs=out_specs, check_vma=False
    )
```

```python
import math

import jax
import jax.numpy as jnp
from jax import lax
from jax.sharding import PartitionSpec as P


F32 = jnp.float32
BF16 = jnp.bfloat16


DOM = ("zdom", "core")
ALL = ("group",) + DOM
CHIP = ("group", "zdom")


def size_of(axes):
    return math.prod(lax.axis_size(axis) for axis in axes)


def extended(block, sides, width):
    for axis, dim in sides:
        count = size_of(axis)
        forward = [(i, i + 1) for i in range(count - 1)]
        backward = [(target, source) for source, target in forward]
        low = lax.ppermute(
            lax.slice_in_dim(block, block.shape[dim] - width, None, axis=dim), axis, forward
        )
        high = lax.ppermute(lax.slice_in_dim(block, 0, width, axis=dim), axis, backward)
        block = jnp.concatenate([low, block, high], axis=dim)
    return block


def silu_slope(values):
    sigma_val = jax.nn.sigmoid(values)
    return sigma_val * (1.0 + values * (1.0 - sigma_val))


def one_hot(index, count):
    return (index[..., None] == jnp.arange(count, dtype=index.dtype)).astype(BF16)


def one_hot_rows(index, count):
    return (jnp.arange(count, dtype=index.dtype)[:, None] == index[..., None, :]).astype(BF16)


def split_dot(spec, left, right):
    return jnp.einsum(
        spec, left, right.astype(F32), precision=lax.Precision.HIGHEST, preferred_element_type=F32
    )


def all_sum(rows, owners):
    count, width = rows.shape
    chips = size_of(CHIP)
    cores = lax.axis_size("core")
    unit = chips * cores * 8
    length = -(-count // unit) * unit
    rows = jnp.pad(rows, ((0, length - count), (0, 0))).reshape(cores, length // cores, width)
    core = lax.axis_index("core")
    swap = [(i, (i + 1) % cores) for i in range(cores)]
    kept = jnp.where(core == 0, rows[0], rows[1])
    given = jnp.where(core == 0, rows[1], rows[0])
    half = kept + lax.ppermute(given.astype(BF16), "core", swap).astype(F32)
    mine = lax.all_to_all(
        half.astype(BF16).reshape(chips, -1, width), CHIP, split_axis=0, concat_axis=0, tiled=True
    )
    mine = jnp.einsum(
        "o,orw->rw", jnp.ones((chips,), BF16), mine, preferred_element_type=F32
    ).astype(BF16)
    spread = jnp.broadcast_to(mine[None], (chips,) + mine.shape)
    own_half = lax.all_to_all(spread, CHIP, split_axis=0, concat_axis=0, tiled=True).reshape(
        -1, width
    )
    other_half = lax.ppermute(own_half, "core", swap)
    first = jnp.where(core == 0, own_half, other_half)
    second = jnp.where(core == 0, other_half, own_half)
    return jnp.concatenate([first, second], 0)[:count].astype(F32)


def on_device(
    pin_feats,
    w_self,
    w_edge,
    w_head,
    w_out,
    send_rows,
    edge_src,
    edge_dst,
    pin_owner,
    pin_net,
    net_target,
):
    pin_count, feat_width = pin_feats.shape
    send_list = send_rows[0]
    halo_span = send_list.shape[0] // 2
    send_hot = one_hot(send_list, pin_count)
    outgoing = jnp.dot(send_hot, pin_feats, preferred_element_type=F32).astype(BF16)
    padded = extended(outgoing, ((DOM, 0),), halo_span)
    node_table = jnp.concatenate([pin_feats, padded[:halo_span], padded[3 * halo_span :]], 0)
    table_rows = node_table.shape[0]
    sources = edge_src[0]
    endpoints = edge_dst[0]
    src_hot = one_hot(sources, table_rows)
    dst_hot = one_hot(endpoints, pin_count)
    gathered = jnp.einsum(
        "ter,rd->ted", src_hot, node_table, preferred_element_type=F32
    ).astype(BF16)
    edge_in = jnp.einsum(
        "tpe,ted->tpd", one_hot_rows(endpoints, pin_count), gathered, preferred_element_type=F32
    )
    summed = split_dot("tpk,tkd->pd", edge_in, w_edge)
    degree = jnp.sum(dst_hot.astype(F32), axis=(0, 1))
    inverse = 1.0 / (1.0 + degree)
    preact = (
        jnp.dot(pin_feats, w_self, preferred_element_type=F32) + summed * inverse[:, None]
    )
    hidden = jax.nn.silu(preact).astype(BF16)
    groups = lax.axis_size("group")
    domains = size_of(DOM)
    owners = groups * domains
    capacity = max(2, 2 * pin_count // owners)
    net_count = net_target.shape[0]
    owner_ids = pin_owner[:, 0]
    owner_hot = one_hot(owner_ids, owners)
    earlier = (
        jnp.arange(pin_count, dtype=jnp.int32)[None, :]
        < jnp.arange(pin_count, dtype=jnp.int32)[:, None]
    ).astype(BF16)
    before = jnp.dot(earlier, owner_hot, preferred_element_type=F32)
    slot_rank = jnp.sum(before * owner_hot.astype(F32), axis=1).astype(jnp.int32)
    pin_slot = owner_ids * capacity + slot_rank
    slot_hot = one_hot(pin_slot, owners * capacity)
    net_code = (pin_net + 1).astype(BF16)[:, None]
    slot_rows = one_hot_rows(pin_slot, owners * capacity)
    slot_nets = jnp.dot(slot_rows, net_code, preferred_element_type=F32)[:, 0] - 1.0
    outbound = jnp.dot(slot_rows, hidden, preferred_element_type=F32).astype(BF16)
    id_rows = -(-capacity // (8 * feat_width)) * 8
    id_block = jnp.pad(
        slot_nets.reshape(owners, capacity), ((0, 0), (0, id_rows * feat_width - capacity))
    ).astype(BF16)
    packet = jnp.concatenate(
        [
            outbound.reshape(owners, capacity, feat_width),
            id_block.reshape(owners, id_rows, feat_width),
        ],
        1,
    )
    packet_in = lax.all_to_all(packet, ALL, split_axis=0, concat_axis=0, tiled=True)
    inbound = packet_in[:, :capacity].reshape(-1, feat_width)
    slot_nets_in = (
        packet_in[:, capacity:].reshape(owners, -1)[:, :capacity].astype(F32).astype(jnp.int32)
    ).reshape(-1)
    net_hot = one_hot(slot_nets_in, net_count)
    pooled = jnp.dot(
        one_hot_rows(slot_nets_in, net_count), inbound, preferred_element_type=F32
    )
    pooled_b = pooled.astype(BF16)
    head_pre = jnp.dot(pooled_b, w_head, preferred_element_type=F32)
    activated = jax.nn.silu(head_pre).astype(BF16)
    predicted = jnp.dot(activated, w_out, preferred_element_type=F32)
    misfit = predicted - net_target
    head_grad = (
        misfit[:, None] * w_out.astype(F32)[None, :] * silu_slope(head_pre)
    ).astype(BF16)
    head_sum_t = jnp.einsum("nh,nd->hd", head_grad, pooled_b, preferred_element_type=F32)
    out_sum = jnp.dot(misfit, activated.astype(F32), precision=lax.Precision.HIGHEST)
    net_grad = jnp.einsum(
        "nh,dh->nd", head_grad, w_head, preferred_element_type=F32
    ).astype(BF16)
    returned = jnp.dot(net_hot, net_grad, preferred_element_type=F32).astype(BF16)
    out_rows = out_sum.reshape(-1, feat_width).astype(BF16)
    back_rows = -(-(capacity + out_rows.shape[0]) // 8) * 8
    back_packet = jnp.concatenate(
        [
            returned.reshape(owners, capacity, feat_width),
            jnp.broadcast_to(out_rows[None], (owners,) + out_rows.shape),
            jnp.zeros(
                (owners, back_rows - capacity - out_rows.shape[0], feat_width), BF16
            ),
        ],
        1,
    )
    back_in = lax.all_to_all(
        back_packet, ALL, split_axis=0, concat_axis=0, tiled=True
    )
    arrived = back_in[:, :capacity].reshape(-1, feat_width)
    out_total = jnp.einsum(
        "o,orw->rw",
        jnp.ones((owners,), BF16),
        back_in[:, capacity : capacity + out_rows.shape[0]],
        preferred_element_type=F32,
    ).reshape(-1)
    pin_grad = jnp.dot(slot_hot, arrived, preferred_element_type=F32)
    preact_grad = (pin_grad * silu_slope(preact)).astype(BF16)
    self_sum = jnp.einsum("pk,pd->kd", pin_feats, preact_grad, preferred_element_type=F32)
    agg_grad = (preact_grad.astype(F32) * inverse[:, None]).astype(BF16)
    edge_rows = jnp.einsum(
        "tep,pd->ted", dst_hot, agg_grad, preferred_element_type=F32
    ).astype(BF16)
    edge_sum = jnp.einsum("tek,ted->tkd", gathered, edge_rows, preferred_element_type=F32)
    row_in = jnp.einsum(
        "tre,ted->trd", one_hot_rows(sources, table_rows), edge_rows, preferred_element_type=F32
    )
    table_grad = split_dot("trd,tkd->rk", row_in, w_edge)
    local_grad = (
        jnp.einsum("pd,kd->pk", preact_grad, w_self, preferred_element_type=F32)
        + table_grad[:pin_count]
    )
    halo_grad = table_grad[pin_count:].astype(BF16)
    back_padded = extended(halo_grad, ((DOM, 0),), halo_span)
    received = jnp.concatenate([back_padded[:halo_span], back_padded[3 * halo_span :]], 0)
    grad_feats = (
        local_grad
        + jnp.dot(one_hot_rows(send_list, pin_count), received, preferred_element_type=F32)
    ).astype(BF16)
    pieces = (self_sum, edge_sum.reshape(-1, feat_width), head_sum_t)
    totals = all_sum(jnp.concatenate(pieces, 0), owners)
    grad_scale = 1.0 / math.sqrt(pin_count * owners)
    outs = []
    offset = 0
    for piece in pieces:
        outs.append(totals[offset : offset + piece.shape[0]] * grad_scale)
        offset += piece.shape[0]
    return (
        predicted,
        grad_feats,
        outs[0],
        outs[1].reshape(edge_sum.shape),
        outs[2].T,
        out_total * grad_scale,
    )


def solution(mesh):
    in_specs = (
        P(ALL, None),
        P(),
        P(),
        P(),
        P(),
        P(ALL, None),
        P(ALL, None, None),
        P(ALL, None, None),
        P(ALL, None),
        P(ALL),
        P(ALL),
    )
    out_specs = (P(ALL), P(ALL, None), P(), P(), P(), P())
    shape = mesh.devices.shape
    cores = 2
    chip_mesh = jax.sharding.Mesh(
        mesh.devices.reshape(shape[0], shape[1] // cores, cores), ("group", "zdom", "core")
    )
    return jax.shard_map(
        on_device, mesh=chip_mesh, in_specs=in_specs, out_specs=out_specs, check_vma=False
    )
```

```python
import math

import jax
import jax.numpy as jnp
from jax import lax
from jax.sharding import PartitionSpec as P


F32 = jnp.float32
BF16 = jnp.bfloat16


DOM = ("zdom", "core")
ALL = ("group",) + DOM
CHIP = ("group", "zdom")


def size_of(axes):
    return math.prod(lax.axis_size(axis) for axis in axes)


def extended(block, sides, width):
    for axis, dim in sides:
        count = size_of(axis)
        forward = [(i, i + 1) for i in range(count - 1)]
        backward = [(target, source) for source, target in forward]
        low = lax.ppermute(
            lax.slice_in_dim(block, block.shape[dim] - width, None, axis=dim), axis, forward
        )
        high = lax.ppermute(lax.slice_in_dim(block, 0, width, axis=dim), axis, backward)
        block = jnp.concatenate([low, block, high], axis=dim)
    return block


def silu_slope(values):
    sigma_val = jax.nn.sigmoid(values)
    return sigma_val * (1.0 + values * (1.0 - sigma_val))


def one_hot(index, count):
    return (index[..., None] == jnp.arange(count, dtype=index.dtype)).astype(BF16)


def one_hot_rows(index, count):
    return (jnp.arange(count, dtype=index.dtype)[:, None] == index[..., None, :]).astype(BF16)


def split_dot(spec, left, right):
    return jnp.einsum(
        spec, left, right.astype(F32), precision=lax.Precision.HIGHEST, preferred_element_type=F32
    )


def all_sum(rows, owners):
    count, width = rows.shape
    chips = size_of(CHIP)
    cores = lax.axis_size("core")
    unit = chips * cores * 8
    length = -(-count // unit) * unit
    rows = jnp.pad(rows, ((0, length - count), (0, 0))).reshape(cores, length // cores, width)
    core = lax.axis_index("core")
    swap = [(i, (i + 1) % cores) for i in range(cores)]
    kept = jnp.where(core == 0, rows[0], rows[1])
    given = jnp.where(core == 0, rows[1], rows[0])
    half = kept + lax.ppermute(given.astype(BF16), "core", swap).astype(F32)
    mine = lax.all_to_all(
        half.astype(BF16).reshape(chips, -1, width), CHIP, split_axis=0, concat_axis=0, tiled=True
    )
    mine = jnp.einsum(
        "o,orw->rw", jnp.ones((chips,), BF16), mine, preferred_element_type=F32
    ).astype(BF16)
    spread = jnp.broadcast_to(mine[None], (chips,) + mine.shape)
    own_half = lax.all_to_all(spread, CHIP, split_axis=0, concat_axis=0, tiled=True).reshape(
        -1, width
    )
    other_half = lax.ppermute(own_half, "core", swap)
    first = jnp.where(core == 0, own_half, other_half)
    second = jnp.where(core == 0, other_half, own_half)
    return jnp.concatenate([first, second], 0)[:count].astype(F32)


def on_device(
    pin_feats,
    w_self,
    w_edge,
    w_head,
    w_out,
    send_rows,
    edge_src,
    edge_dst,
    pin_owner,
    pin_net,
    net_target,
):
    pin_count, feat_width = pin_feats.shape
    send_list = send_rows[0]
    halo_span = send_list.shape[0] // 2
    send_hot = one_hot(send_list, pin_count)
    outgoing = jnp.dot(send_hot, pin_feats, preferred_element_type=F32).astype(BF16)
    padded = extended(outgoing, ((DOM, 0),), halo_span)
    node_table = jnp.concatenate([pin_feats, padded[:halo_span], padded[3 * halo_span :]], 0)
    table_rows = node_table.shape[0]
    sources = edge_src[0]
    endpoints = edge_dst[0]
    src_hot = one_hot(sources, table_rows)
    dst_hot = one_hot(endpoints, pin_count)
    gathered = jnp.einsum(
        "ter,rd->ted", src_hot, node_table, preferred_element_type=F32
    ).astype(BF16)
    dst_rows = one_hot_rows(endpoints, pin_count)
    edge_in = jnp.einsum("tpe,ted->tpd", dst_rows, gathered, preferred_element_type=F32)
    summed = split_dot("tpk,tkd->pd", edge_in, w_edge)
    degree = jnp.sum(dst_rows.astype(F32), axis=(0, 2))
    inverse = 1.0 / (1.0 + degree)
    preact = (
        jnp.dot(pin_feats, w_self, preferred_element_type=F32) + summed * inverse[:, None]
    )
    hidden = jax.nn.silu(preact).astype(BF16)
    groups = lax.axis_size("group")
    domains = size_of(DOM)
    owners = groups * domains
    capacity = max(2, 2 * pin_count // owners)
    net_count = net_target.shape[0]
    owner_ids = pin_owner[:, 0]
    owner_hot = one_hot(owner_ids, owners)
    earlier = (
        jnp.arange(pin_count, dtype=jnp.int32)[None, :]
        < jnp.arange(pin_count, dtype=jnp.int32)[:, None]
    ).astype(BF16)
    before = jnp.dot(earlier, owner_hot, preferred_element_type=F32)
    slot_rank = jnp.sum(before * owner_hot.astype(F32), axis=1).astype(jnp.int32)
    pin_slot = owner_ids * capacity + slot_rank
    slot_hot = one_hot(pin_slot, owners * capacity)
    net_code = (pin_net + 1).astype(BF16)[:, None]
    slot_rows = one_hot_rows(pin_slot, owners * capacity)
    slot_nets = jnp.dot(slot_rows, net_code, preferred_element_type=F32)[:, 0] - 1.0
    outbound = jnp.dot(slot_rows, hidden, preferred_element_type=F32).astype(BF16)
    id_rows = -(-capacity // (8 * feat_width)) * 8
    id_block = jnp.pad(
        slot_nets.reshape(owners, capacity), ((0, 0), (0, id_rows * feat_width - capacity))
    ).astype(BF16)
    packet = jnp.concatenate(
        [
            outbound.reshape(owners, capacity, feat_width),
            id_block.reshape(owners, id_rows, feat_width),
        ],
        1,
    )
    packet_in = lax.all_to_all(packet, ALL, split_axis=0, concat_axis=0, tiled=True)
    inbound = packet_in[:, :capacity].reshape(-1, feat_width)
    slot_nets_in = (
        packet_in[:, capacity:].reshape(owners, -1)[:, :capacity].astype(F32).astype(jnp.int32)
    ).reshape(-1)
    net_hot = one_hot(slot_nets_in, net_count)
    pooled = jnp.dot(
        one_hot_rows(slot_nets_in, net_count), inbound, preferred_element_type=F32
    )
    pooled_b = pooled.astype(BF16)
    head_pre = jnp.dot(pooled_b, w_head, preferred_element_type=F32)
    activated = jax.nn.silu(head_pre).astype(BF16)
    predicted = jnp.dot(activated, w_out, preferred_element_type=F32)
    misfit = predicted - net_target
    head_grad = (
        misfit[:, None] * w_out.astype(F32)[None, :] * silu_slope(head_pre)
    ).astype(BF16)
    head_sum_t = jnp.einsum("nh,nd->hd", head_grad, pooled_b, preferred_element_type=F32)
    out_sum = jnp.dot(misfit, activated.astype(F32), precision=lax.Precision.HIGHEST)
    net_grad = jnp.einsum(
        "nh,dh->nd", head_grad, w_head, preferred_element_type=F32
    ).astype(BF16)
    returned = jnp.dot(net_hot, net_grad, preferred_element_type=F32).astype(BF16)
    out_rows = out_sum.reshape(-1, feat_width).astype(BF16)
    back_rows = -(-(capacity + out_rows.shape[0]) // 8) * 8
    back_packet = jnp.concatenate(
        [
            returned.reshape(owners, capacity, feat_width),
            jnp.broadcast_to(out_rows[None], (owners,) + out_rows.shape),
            jnp.zeros(
                (owners, back_rows - capacity - out_rows.shape[0], feat_width), BF16
            ),
        ],
        1,
    )
    back_in = lax.all_to_all(
        back_packet, ALL, split_axis=0, concat_axis=0, tiled=True
    )
    arrived = back_in[:, :capacity].reshape(-1, feat_width)
    out_total = jnp.einsum(
        "o,orw->rw",
        jnp.ones((owners,), BF16),
        back_in[:, capacity : capacity + out_rows.shape[0]],
        preferred_element_type=F32,
    ).reshape(-1)
    pin_grad = jnp.dot(slot_hot, arrived, preferred_element_type=F32)
    preact_grad = (pin_grad * silu_slope(preact)).astype(BF16)
    self_sum = jnp.einsum("pk,pd->kd", pin_feats, preact_grad, preferred_element_type=F32)
    agg_grad = (preact_grad.astype(F32) * inverse[:, None]).astype(BF16)
    edge_rows = jnp.einsum(
        "tep,pd->ted", dst_hot, agg_grad, preferred_element_type=F32
    ).astype(BF16)
    edge_sum = jnp.einsum("tek,ted->tkd", gathered, edge_rows, preferred_element_type=F32)
    row_in = jnp.einsum(
        "tre,ted->trd", one_hot_rows(sources, table_rows), edge_rows, preferred_element_type=F32
    )
    table_grad = split_dot("trd,tkd->rk", row_in, w_edge)
    local_grad = (
        jnp.einsum("pd,kd->pk", preact_grad, w_self, preferred_element_type=F32)
        + table_grad[:pin_count]
    )
    halo_grad = table_grad[pin_count:].astype(BF16)
    back_padded = extended(halo_grad, ((DOM, 0),), halo_span)
    received = jnp.concatenate([back_padded[:halo_span], back_padded[3 * halo_span :]], 0)
    grad_feats = (
        local_grad
        + jnp.dot(one_hot_rows(send_list, pin_count), received, preferred_element_type=F32)
    ).astype(BF16)
    pieces = (self_sum, edge_sum.reshape(-1, feat_width), head_sum_t)
    totals = all_sum(jnp.concatenate(pieces, 0), owners)
    grad_scale = 1.0 / math.sqrt(pin_count * owners)
    outs = []
    offset = 0
    for piece in pieces:
        outs.append(totals[offset : offset + piece.shape[0]] * grad_scale)
        offset += piece.shape[0]
    return (
        predicted,
        grad_feats,
        outs[0],
        outs[1].reshape(edge_sum.shape),
        outs[2].T,
        out_total * grad_scale,
    )


def solution(mesh):
    in_specs = (
        P(ALL, None),
        P(),
        P(),
        P(),
        P(),
        P(ALL, None),
        P(ALL, None, None),
        P(ALL, None, None),
        P(ALL, None),
        P(ALL),
        P(ALL),
    )
    out_specs = (P(ALL), P(ALL, None), P(), P(), P(), P())
    shape = mesh.devices.shape
    cores = 2
    chip_mesh = jax.sharding.Mesh(
        mesh.devices.reshape(shape[0], shape[1] // cores, cores), ("group", "zdom", "core")
    )
    return jax.shard_map(
        on_device, mesh=chip_mesh, in_specs=in_specs, out_specs=out_specs, check_vma=False
    )
```
